512 devices in a mesh: ctx: 32 (over x, y), head: 16 (over z, core).
Axes of the slice: x: 4, y: 8, z: 8, core: 2. Of those that a mesh axis runs over, the one named last changes fastest.
Arguments:
- q_soft: bfloat16 [16384, 4096], P(('ctx', 'head')), may hold values from -5 to 5
- k_soft: bfloat16 [16384, 4096], P(('ctx', 'head')), may hold values from -5 to 5
- v_soft: bfloat16 [16384, 4096], P(('ctx', 'head')), may hold values from -6 to 6
- q_light: bfloat16 [16384, 4096], P(('ctx', 'head')), may hold values from -6 to 6
- k_light: bfloat16 [16384, 4096], P(('ctx', 'head')), may hold values from -6 to 6
- v_light: bfloat16 [16384, 4096], P(('ctx', 'head')), may hold values from -100 to 100
- decay_log: float32 [32, 16384], P('head', 'ctx'), may hold values from -1 to 0
- norm_gain: float32 [4096], P('head'), may hold values from 0.5 to 1.5
- doc_lengths: int32 [32], replicated, may hold values from 1 to 4096, 16384 in all
Outputs:
- attn_soft: bfloat16 [16384, 4096], P(('ctx', 'head'))
- attn_light: bfloat16 [16384, 4096], P(('ctx', 'head'))
The draws below stay inside these ranges and needn't reach their ends.
Inputs may be any that keep to these rules, and one draw needn't show every extreme that they name: `doc_lengths`: the lengths sum to 16384; the largest is exactly 4096.
All inputs are finite; a program needn't handle non-finite values.
Results may differ from the reference program's by a relative error of at most 0.013.
Values may be sent and summed in bfloat16 or wider, within the bound.
No kernel may reach another device: no remote copies, remote signals or barrier semaphores. Data moves between devices by JAX's collectives and lax.ppermute only.
A program may use at most 64 MiB of HBM per device.

```python
import math
import jax
import jax.numpy as jnp
import numpy as np
from jax import lax

DH = 128
TOK_DEV = 512
HEAD_TOTAL = 32
TOKEN_TOTAL = 16384
DOC_SHARDS = 8
DOC_MAX = 4096
NDOC = 32


def base_values(key, salt):
    drawn = jax.random.normal(jax.random.fold_in(key, salt), (TOKEN_TOTAL, HEAD_TOTAL * DH), jnp.float32)
    return jnp.clip(drawn, -5.0, 5.0)


def draw_q_soft(key, part):
    values_drawn = base_values(key, 1)
    return values_drawn.astype(jnp.bfloat16)


def draw_k_soft(key, part):
    values_drawn = base_values(key, 2)
    return values_drawn.astype(jnp.bfloat16)


def draw_v_light(key, part):
    row_scale = jnp.exp(jax.random.uniform(jax.random.fold_in(key, 5), (TOKEN_TOTAL, 1), jnp.float32, 0.0, 2.302585))
    col_scale = jnp.exp(jax.random.uniform(jax.random.fold_in(key, 6), (1, HEAD_TOTAL * DH), jnp.float32, 0.0, 2.302585))
    noise = jnp.clip(jax.random.normal(jax.random.fold_in(key, 9), (TOKEN_TOTAL, HEAD_TOTAL * DH), jnp.float32), -4.0, 4.0)
    values_drawn = noise * row_scale * col_scale / 4.0
    return values_drawn.astype(jnp.bfloat16)


def draw_decay_log(key, part):
    fast_share = 0.5
    fast_heads = jax.random.bernoulli(jax.random.fold_in(key, 31), fast_share, (HEAD_TOTAL, 1))
    slow_total = jax.random.uniform(jax.random.fold_in(key, 32), (HEAD_TOTAL, 1), jnp.float32, 0.2, 0.8)
    fast_rate = jax.random.uniform(jax.random.fold_in(key, 33), (HEAD_TOTAL, 1), jnp.float32, 1.0 / 50.0, 1.0 / 30.0)
    decay_rate_floor = jnp.where(fast_heads, fast_rate, slow_total / TOKEN_TOTAL)
    block_count = TOKEN_TOTAL // TOK_DEV
    block_multiplier = jnp.exp(jax.random.uniform(jax.random.fold_in(key, 34), (HEAD_TOTAL, block_count, 1), jnp.float32, -0.7, 0.7))
    block_multiplier = jnp.broadcast_to(block_multiplier, (HEAD_TOTAL, block_count, TOK_DEV)).reshape(HEAD_TOTAL, TOKEN_TOTAL)
    coarse_estimate = jnp.exp(jax.random.uniform(jax.random.fold_in(key, 35), (HEAD_TOTAL, TOKEN_TOTAL), jnp.float32, -0.7, 0.7))
    segment_blocks = jax.random.bernoulli(jax.random.fold_in(key, 36), 2.0 / TOKEN_TOTAL, (HEAD_TOTAL, TOKEN_TOTAL)).astype(jnp.float32)
    segment_length = jax.random.uniform(jax.random.fold_in(key, 37), (HEAD_TOTAL, TOKEN_TOTAL), jnp.float32, 0.22, 0.69)
    return -decay_rate_floor * block_multiplier * coarse_estimate - segment_blocks * segment_length


def levels(own_key, extent, shards, low, high):
    loudness, own = 1.0, jax.random.fold_in(own_key, 6)
    for dim, parts in shards:
        steps = jnp.exp(jax.random.uniform(jax.random.fold_in(own, dim), (parts,), jnp.float32, low / len(shards), high / len(shards)))
        loudness = loudness * jnp.repeat(steps, extent[dim] // parts).reshape([-1 if axis == dim else 1 for axis in range(len(extent))])
    return loudness


def profile(amount, total, limit, slope):
    portions = [(1 << 20) // math.isqrt(rank ** slope) + 1 for rank in range(2, amount + 1)]
    rest, counts = total - limit - (amount - 1), [1] * (amount - 1)
    while rest > 0:
        free = [i for i in range(amount - 1) if counts[i] < limit]
        mass, left = sum([portions[i] for i in free]), rest
        for i in free:
            addition = min(limit - counts[i], max(1, left * portions[i] // mass), rest)
            counts[i] = counts[i] + addition
            rest = rest - addition
    return np.array([limit] + counts)


def ragged_sizes(own_key, number_of, total, most, skew):
    if number_of == 2:
        one = jax.random.randint(own_key, (), max(1, total - most), min(most, total - 1) + 1)
        return jnp.stack([one, total - one])
    tallies = jnp.asarray(profile(number_of, total, most, skew), jnp.int32)
    pairs = (number_of - 1) // 2
    donor, taker = tallies[1:1 + 2 * pairs:2], tallies[2:2 + 2 * pairs:2]
    room = jnp.minimum(donor - 1, most - taker)
    shifted = jax.random.randint(jax.random.fold_in(own_key, 1), (pairs,), 0, 1 << 20) % (room + 1)
    tallies = tallies.at[1:1 + 2 * pairs:2].set(donor - shifted).at[2:2 + 2 * pairs:2].set(taker + shifted)
    return tallies[jax.random.permutation(jax.random.fold_in(own_key, 2), number_of)]


def scatter_about(key, dims, deviation, most, pieces=(), kind=jnp.bfloat16):
    level = levels(key, dims, pieces, -0.22, 0.18) if pieces else 1.0
    values = jax.random.normal(key, dims, jnp.float32) * deviation * level
    return jnp.minimum(jnp.maximum(values, -most), most).astype(kind)


def setup_inputs(seed: int = 0) -> dict:
    splits = jax.random.split(jax.random.key(seed), 10)
    return {
        "q_soft": draw_q_soft(jax.random.fold_in(splits[9], 71), 0),
        "k_soft": draw_k_soft(jax.random.fold_in(splits[9], 71), 0),
        "v_soft": scatter_about(splits[2], (TOKEN_TOTAL, HEAD_TOTAL * DH), 1.0, 6.0, ((0, 512),)),
        "q_light": scatter_about(splits[3], (TOKEN_TOTAL, HEAD_TOTAL * DH), 1.0, 6.0, ((0, 512),)),
        "k_light": scatter_about(splits[4], (TOKEN_TOTAL, HEAD_TOTAL * DH), 1.0, 6.0, ((0, 512),)),
        "v_light": draw_v_light(jax.random.fold_in(splits[9], 71), 0),
        "decay_log": draw_decay_log(jax.random.fold_in(splits[9], 71), 0),
        "norm_gain": jnp.clip(1.0 + 0.1 * jax.random.normal(splits[7], (HEAD_TOTAL * DH,), jnp.float32), 0.5, 1.5),
        "doc_lengths": ragged_sizes(splits[8], NDOC, TOKEN_TOTAL, DOC_MAX, 2).astype(jnp.int32),
    }


def doc_index(positions, starts):
    return lax.optimization_barrier(jnp.sum((positions[:, None] >= starts[None, :]).astype(jnp.int32), axis=1)) - 1

def reference(q_soft, k_soft, v_soft, q_light, k_light, v_light, decay_log, norm_gain, doc_lengths):
    starts = jnp.cumsum(doc_lengths) - doc_lengths
    blocks = TOKEN_TOTAL // TOK_DEV
    padding = DOC_SHARDS * TOK_DEV
    window = (DOC_SHARDS + 1) * TOK_DEV
    score_scale = 1.0 / DH ** 0.5
    queries = q_soft.reshape(blocks, TOK_DEV, HEAD_TOTAL, DH).transpose(0, 2, 1, 3)
    keys_pad = jnp.concatenate([jnp.zeros((padding, HEAD_TOTAL * DH), k_soft.dtype), k_soft]).reshape(-1, HEAD_TOTAL, DH).transpose(1, 0, 2)
    vals_pad = jnp.concatenate([jnp.zeros((padding, HEAD_TOTAL * DH), v_soft.dtype), v_soft]).reshape(-1, HEAD_TOTAL, DH).transpose(1, 0, 2)

    def soft_item(item_index):
        block_index = item_index // HEAD_TOTAL
        head_index = item_index % HEAD_TOTAL
        query_rows = queries[block_index, head_index].astype(jnp.float32)
        key_rows = lax.dynamic_slice_in_dim(keys_pad[head_index], block_index * TOK_DEV, window, 0).astype(jnp.float32)
        val_rows = lax.dynamic_slice_in_dim(vals_pad[head_index], block_index * TOK_DEV, window, 0).astype(jnp.float32)
        query_pos = block_index * TOK_DEV + jnp.arange(TOK_DEV, dtype=jnp.int32)
        key_pos = block_index * TOK_DEV - padding + jnp.arange(window, dtype=jnp.int32)
        allowed = (doc_index(query_pos, starts)[:, None] == doc_index(key_pos, starts)[None, :]) & (key_pos[None, :] <= query_pos[:, None])
        scores = jnp.einsum('td,sd->ts', query_rows, key_rows, precision=lax.Precision.HIGHEST) * score_scale
        scores = jnp.where(allowed, scores, -jnp.inf)
        row_max = lax.optimization_barrier(jnp.max(scores, axis=1, keepdims=True))
        probs = jnp.exp(scores - row_max)
        totals = lax.optimization_barrier(jnp.sum(probs, axis=1, keepdims=True))
        probs_low = lax.optimization_barrier(probs.astype(jnp.bfloat16)).astype(jnp.float32)
        mixed = jnp.einsum('ts,sd->td', probs_low, val_rows, precision=lax.Precision.HIGHEST) / totals
        return mixed.astype(jnp.bfloat16)
    soft_items = lax.map(soft_item, jnp.arange(blocks * HEAD_TOTAL, dtype=jnp.int32))
    attn_soft = soft_items.reshape(blocks, HEAD_TOTAL, TOK_DEV, DH).transpose(0, 2, 1, 3).reshape(TOKEN_TOTAL, HEAD_TOTAL * DH)
    light_q = q_light.reshape(blocks, TOK_DEV, HEAD_TOTAL, DH)
    light_k = k_light.reshape(blocks, TOK_DEV, HEAD_TOTAL, DH)
    light_v = v_light.reshape(blocks, TOK_DEV, HEAD_TOTAL, DH)
    light_decay = decay_log.reshape(HEAD_TOTAL, blocks, TOK_DEV).transpose(1, 0, 2)
    gains = norm_gain.reshape(HEAD_TOTAL, DH)[None]
    token_ids = jnp.arange(TOK_DEV, dtype=jnp.int32)
    causal = token_ids[None, :] <= token_ids[:, None]

    def light_step(carried, inputs):
        query_blk, key_blk, val_blk, decay_blk = inputs
        cumul = jnp.cumsum(decay_blk, axis=1)
        block_end = cumul[:, -1:]
        query_f = query_blk.astype(jnp.float32)
        key_f = key_blk.astype(jnp.float32)
        val_f = val_blk.astype(jnp.float32)
        log_gap = jnp.where(causal[None], cumul[:, :, None] - cumul[:, None, :], -jnp.inf)
        raw_scores = jnp.einsum('thd,shd->hts', query_f, key_f, precision=lax.Precision.HIGHEST)
        gated = lax.optimization_barrier((raw_scores * jnp.exp(log_gap)).astype(jnp.bfloat16)).astype(jnp.float32)
        inner = jnp.einsum('hts,shd->thd', gated, val_f, precision=lax.Precision.HIGHEST)
        state_low = lax.optimization_barrier(carried.astype(jnp.bfloat16)).astype(jnp.float32)
        outer = jnp.einsum('thd,hde->the', query_f, state_low, precision=lax.Precision.HIGHEST) * jnp.exp(cumul).T[:, :, None]
        raw_out = inner + outer
        mean_sq = lax.optimization_barrier(jnp.mean(raw_out * raw_out, axis=2, keepdims=True))
        normed = raw_out / jnp.sqrt(mean_sq + 1e-06) * gains
        weighted = lax.optimization_barrier((key_f * jnp.exp(block_end - cumul).T[:, :, None]).astype(jnp.bfloat16)).astype(jnp.float32)
        update = jnp.einsum('thd,the->hde', weighted, val_f, precision=lax.Precision.HIGHEST)
        next_state = jnp.exp(block_end[:, 0])[:, None, None] * carried + update
        return (next_state, normed.astype(jnp.bfloat16).reshape(TOK_DEV, HEAD_TOTAL * DH))
    start_state = jnp.zeros((HEAD_TOTAL, DH, DH), jnp.float32)
    final_state, light_out = lax.scan(light_step, start_state, (light_q, light_k, light_v, light_decay))
    attn_light = light_out.reshape(TOKEN_TOTAL, HEAD_TOTAL * DH)
    return (attn_soft, attn_light)
```

```python
from functools import partial

import jax
import jax.numpy as jnp
from jax import lax
from jax.sharding import PartitionSpec as P

DOC_REACH = 8


def shifted(block, axis, distance):
    size = lax.axis_size(axis)
    route = [(i, (i + distance) % size) for i in range(size)]
    return lax.ppermute(block, axis, route)


def doc_index(positions, starts):
    return jnp.sum((positions[:, None] >= starts[None, :]).astype(jnp.int32), axis=1) - 1


def absorb_block(
    running,
    kv_pair,
    source,
    queries,
    query_pos,
    query_doc,
    starts,
    row_count,
    heads_dev,
    head_width,
):
    key_block = kv_pair[0].reshape(row_count, heads_dev, head_width)
    val_block = kv_pair[1].reshape(row_count, heads_dev, head_width)
    key_pos = source * row_count + jnp.arange(row_count, dtype=jnp.int32)
    key_doc = doc_index(key_pos, starts)
    allowed = (query_doc[:, None] == key_doc[None, :]) & (key_pos[None, :] <= query_pos[:, None])
    scores = (
        jnp.einsum("thd,shd->hts", queries, key_block, preferred_element_type=jnp.float32)
        / head_width**0.5
    )
    scores = jnp.where(allowed[None], scores, -1e30)
    run_max, run_total, run_acc = running
    new_max = jnp.maximum(run_max, jnp.max(scores, axis=2))
    correction = jnp.exp(run_max - new_max)
    probs = jnp.where(allowed[None], jnp.exp(scores - new_max[:, :, None]), 0.0)
    new_total = run_total * correction + jnp.sum(probs, axis=2)
    product = jnp.einsum(
        "hts,shd->thd", probs.astype(jnp.bfloat16), val_block, preferred_element_type=jnp.float32
    )
    new_acc = run_acc * correction.T[:, :, None] + product
    return (new_max, new_total, new_acc)


def keep_running(running):
    return running


def soft_attention(q_rows, kv_pair, doc_lengths, row_count, heads_dev, head_width):
    size = lax.axis_size("ctx")
    own_index = lax.axis_index("ctx")
    reach = min(DOC_REACH, size - 1)
    forward_steps = (reach + 1) // 2
    starts = jnp.cumsum(doc_lengths) - doc_lengths
    query_pos = own_index * row_count + jnp.arange(row_count, dtype=jnp.int32)
    query_doc = doc_index(query_pos, starts)
    queries = q_rows.reshape(row_count, heads_dev, head_width)
    absorb = partial(
        absorb_block,
        queries=queries,
        query_pos=query_pos,
        query_doc=query_doc,
        starts=starts,
        row_count=row_count,
        heads_dev=heads_dev,
        head_width=head_width,
    )
    running = (
        jnp.full((heads_dev, row_count), -1e30, jnp.float32),
        jnp.zeros((heads_dev, row_count), jnp.float32),
        jnp.zeros((row_count, heads_dev, head_width), jnp.float32),
    )
    arrivals = []
    ahead = kv_pair
    for offset in range(1, forward_steps + 1):
        ahead = shifted(ahead, "ctx", 1)
        arrivals.append((ahead, offset))
    if reach > forward_steps:
        behind = shifted(kv_pair, "ctx", reach)
        arrivals.append((behind, reach))
        for offset in range(reach - 1, forward_steps, -1):
            behind = shifted(behind, "ctx", -1)
            arrivals.append((behind, offset))
    order = []
    fwd = [a for a in arrivals if a[1] <= forward_steps]
    bwd = [a for a in arrivals if a[1] > forward_steps]
    for i in range(max(len(fwd), len(bwd))):
        if i < len(fwd):
            order.append(fwd[i])
        if i < len(bwd):
            order.append(bwd[i])
    running = absorb(running, kv_pair, own_index)
    for block, offset in order:
        source = own_index - offset
        last_doc = doc_index(jnp.full((1,), source * row_count + row_count - 1, jnp.int32), starts)[
            0
        ]
        needed = (source >= 0) & (last_doc == query_doc[0])
        running = lax.cond(
            needed, partial(absorb, kv_pair=block, source=source), keep_running, running
        )
    run_max, run_total, run_acc = running
    mixed = run_acc / run_total.T[:, :, None]
    return mixed.astype(jnp.bfloat16).reshape(row_count, heads_dev * head_width)


def lightning(q_rows, k_rows, v_rows, decay_log, norm_gain, row_count, heads_dev, head_width):
    size = lax.axis_size("ctx")
    own_index = lax.axis_index("ctx")
    cumul = jnp.cumsum(decay_log, axis=1)
    block_end = cumul[:, -1:]
    queries = q_rows.reshape(row_count, heads_dev, head_width)
    keys_here = k_rows.reshape(row_count, heads_dev, head_width)
    vals_here = v_rows.reshape(row_count, heads_dev, head_width)
    weighted = (keys_here * jnp.exp(block_end - cumul).T[:, :, None]).astype(jnp.bfloat16)
    update = jnp.einsum("thd,the->hde", weighted, vals_here, preferred_element_type=jnp.float32)
    end_hi = block_end.astype(jnp.bfloat16)
    end_lo = (block_end - end_hi.astype(jnp.float32)).astype(jnp.bfloat16)
    extra = jnp.zeros((heads_dev, 16, head_width), jnp.bfloat16)
    extra = extra.at[:, 0, :].set(jnp.broadcast_to(end_hi, (heads_dev, head_width)))
    extra = extra.at[:, 1, :].set(jnp.broadcast_to(end_lo, (heads_dev, head_width)))
    packed = jnp.concatenate([update.astype(jnp.bfloat16), extra], axis=1)
    gathered = lax.all_gather(packed, "ctx")
    ends = gathered[:, :, head_width, 0].astype(jnp.float32) + gathered[
        :, :, head_width + 1, 0
    ].astype(jnp.float32)
    blocks = jnp.arange(size, dtype=jnp.int32)
    between = (blocks[:, None] < blocks[None, :]) & (blocks[None, :] < own_index)
    exponent = jnp.einsum(
        "cb,bh->ch", between.astype(jnp.float32), ends, precision=lax.Precision.HIGHEST
    )
    weight = jnp.where((blocks < own_index)[:, None], jnp.exp(exponent), 0.0)
    entering = jnp.einsum(
        "ch,chde->hde",
        weight,
        gathered[:, :, :head_width, :].astype(jnp.float32),
        precision=lax.Precision.HIGHEST,
    )
    state_low = entering.astype(jnp.bfloat16)
    token_ids = jnp.arange(row_count, dtype=jnp.int32)
    causal = token_ids[None, :] <= token_ids[:, None]
    log_gap = jnp.where(causal[None], cumul[:, :, None] - cumul[:, None, :], -jnp.inf)
    raw_scores = jnp.einsum("thd,shd->hts", queries, keys_here, preferred_element_type=jnp.float32)
    gated = (raw_scores * jnp.exp(log_gap)).astype(jnp.bfloat16)
    inner = jnp.einsum("hts,shd->thd", gated, vals_here, preferred_element_type=jnp.float32)
    outer = (
        jnp.einsum("thd,hde->the", queries, state_low, preferred_element_type=jnp.float32)
        * jnp.exp(cumul).T[:, :, None]
    )
    raw_out = inner + outer
    mean_sq = jnp.mean(raw_out * raw_out, axis=2, keepdims=True)
    normed = raw_out * lax.rsqrt(mean_sq + 1e-06) * norm_gain.reshape(heads_dev, head_width)[None]
    return normed.astype(jnp.bfloat16).reshape(row_count, heads_dev * head_width)


def per_device(
    q_soft, k_soft, v_soft, q_light, k_light, v_light, decay_log, norm_gain, doc_lengths
):
    kv_soft = lax.all_to_all(
        jnp.stack([k_soft, v_soft]), "head", split_axis=2, concat_axis=1, tiled=True
    )
    rest = lax.all_to_all(
        jnp.stack([q_soft, q_light, k_light, v_light]),
        "head",
        split_axis=2,
        concat_axis=1,
        tiled=True,
    )
    heads_dev = decay_log.shape[0]
    row_count = kv_soft.shape[1]
    head_width = kv_soft.shape[2] // heads_dev
    light_out = lightning(
        rest[1], rest[2], rest[3], decay_log, norm_gain, row_count, heads_dev, head_width
    )
    soft_out = soft_attention(rest[0], kv_soft, doc_lengths, row_count, heads_dev, head_width)
    returned = lax.all_to_all(
        jnp.stack([soft_out, light_out]), "head", split_axis=1, concat_axis=2, tiled=True
    )
    return (returned[0], returned[1])


def solution(mesh):
    in_specs = (
        P(("ctx", "head"), None),
        P(("ctx", "head"), None),
        P(("ctx", "head"), None),
        P(("ctx", "head"), None),
        P(("ctx", "head"), None),
        P(("ctx", "head"), None),
        P("head", "ctx"),
        P("head"),
        P(),
    )
    out_specs = (P(("ctx", "head"), None), P(("ctx", "head"), None))
    return jax.shard_map(
        per_device, mesh=mesh, in_specs=in_specs, out_specs=out_specs, check_vma=False
    )
```

```python
from functools import partial

import jax
import jax.numpy as jnp
from jax import lax
from jax.sharding import PartitionSpec as P

DOC_REACH = 8


def shifted(block, axis, distance):
    size = lax.axis_size(axis)
    route = [(i, (i + distance) % size) for i in range(size)]
    return lax.ppermute(block, axis, route)


def doc_index(positions, starts):
    return jnp.sum((positions[:, None] >= starts[None, :]).astype(jnp.int32), axis=1) - 1


def block_partial(
    kv_pair,
    source,
    queries,
    query_pos,
    query_doc,
    starts,
    row_count,
    heads_dev,
    head_width,
):
    key_block = kv_pair[0].reshape(row_count, heads_dev, head_width)
    val_block = kv_pair[1].reshape(row_count, heads_dev, head_width)
    key_pos = source * row_count + jnp.arange(row_count, dtype=jnp.int32)
    key_doc = doc_index(key_pos, starts)
    allowed = (query_doc[:, None] == key_doc[None, :]) & (key_pos[None, :] <= query_pos[:, None])
    scores = (
        jnp.einsum("thd,shd->hts", queries, key_block, preferred_element_type=jnp.float32)
        / head_width**0.5
    )
    scores = jnp.where(allowed[None], scores, -1e30)
    block_max = jnp.max(scores, axis=2)
    probs = jnp.where(allowed[None], jnp.exp(scores - block_max[:, :, None]), 0.0)
    block_total = jnp.sum(probs, axis=2)
    product = jnp.einsum(
        "hts,shd->thd", probs.astype(jnp.bfloat16), val_block, preferred_element_type=jnp.float32
    )
    return (block_max, block_total, product)


def empty_partial(row_count, heads_dev, head_width):
    return (
        jnp.full((heads_dev, row_count), -1e30, jnp.float32),
        jnp.zeros((heads_dev, row_count), jnp.float32),
        jnp.zeros((row_count, heads_dev, head_width), jnp.float32),
    )


def soft_attention(q_rows, kv_pair, doc_lengths, row_count, heads_dev, head_width):
    size = lax.axis_size("ctx")
    own_index = lax.axis_index("ctx")
    reach = min(DOC_REACH, size - 1)
    forward_steps = (reach + 1) // 2
    starts = jnp.cumsum(doc_lengths) - doc_lengths
    query_pos = own_index * row_count + jnp.arange(row_count, dtype=jnp.int32)
    query_doc = doc_index(query_pos, starts)
    queries = q_rows.reshape(row_count, heads_dev, head_width)
    absorb = partial(
        block_partial,
        queries=queries,
        query_pos=query_pos,
        query_doc=query_doc,
        starts=starts,
        row_count=row_count,
        heads_dev=heads_dev,
        head_width=head_width,
    )
    arrivals = []
    ahead = kv_pair
    for offset in range(1, forward_steps + 1):
        ahead = shifted(ahead, "ctx", 1)
        arrivals.append((ahead, offset))
    if reach > forward_steps:
        behind = shifted(kv_pair, "ctx", reach)
        arrivals.append((behind, reach))
        for offset in range(reach - 1, forward_steps, -1):
            behind = shifted(behind, "ctx", -1)
            arrivals.append((behind, offset))
    order = []
    fwd = [a for a in arrivals if a[1] <= forward_steps]
    bwd = [a for a in arrivals if a[1] > forward_steps]
    for i in range(max(len(fwd), len(bwd))):
        if i < len(fwd):
            order.append(fwd[i])
        if i < len(bwd):
            order.append(bwd[i])
    partials = [absorb(kv_pair, source=own_index)]
    skip = partial(empty_partial, row_count, heads_dev, head_width)
    for block, offset in order:
        source = own_index - offset
        last_doc = doc_index(jnp.full((1,), source * row_count + row_count - 1, jnp.int32), starts)[
            0
        ]
        needed = (source >= 0) & (last_doc == query_doc[0])
        partials.append(lax.cond(needed, partial(absorb, block, source=source), skip))
    row_max = partials[0][0]
    for part in partials[1:]:
        row_max = jnp.maximum(row_max, part[0])
    run_total = jnp.zeros_like(row_max)
    run_acc = jnp.zeros_like(partials[0][2])
    for part in partials:
        scale = jnp.exp(part[0] - row_max)
        run_total = run_total + part[1] * scale
        run_acc = run_acc + part[2] * scale.T[:, :, None]
    mixed = run_acc / run_total.T[:, :, None]
    return mixed.astype(jnp.bfloat16).reshape(row_count, heads_dev * head_width)


def lightning(q_rows, k_rows, v_rows, decay_log, norm_gain, row_count, heads_dev, head_width):
    size = lax.axis_size("ctx")
    own_index = lax.axis_index("ctx")
    cumul = jnp.cumsum(decay_log, axis=1)
    block_end = cumul[:, -1:]
    queries = q_rows.reshape(row_count, heads_dev, head_width)
    keys_here = k_rows.reshape(row_count, heads_dev, head_width)
    vals_here = v_rows.reshape(row_count, heads_dev, head_width)
    weighted = (keys_here * jnp.exp(block_end - cumul).T[:, :, None]).astype(jnp.bfloat16)
    update = jnp.einsum("thd,the->hde", weighted, vals_here, preferred_element_type=jnp.float32)
    end_hi = block_end.astype(jnp.bfloat16)
    end_lo = (block_end - end_hi.astype(jnp.float32)).astype(jnp.bfloat16)
    extra = jnp.zeros((heads_dev, 16, head_width), jnp.bfloat16)
    extra = extra.at[:, 0, :].set(jnp.broadcast_to(end_hi, (heads_dev, head_width)))
    extra = extra.at[:, 1, :].set(jnp.broadcast_to(end_lo, (heads_dev, head_width)))
    packed = jnp.concatenate([update.astype(jnp.bfloat16), extra], axis=1)
    gathered = lax.all_gather(packed, "ctx")
    ends = gathered[:, :, head_width, 0].astype(jnp.float32) + gathered[
        :, :, head_width + 1, 0
    ].astype(jnp.float32)
    blocks = jnp.arange(size, dtype=jnp.int32)
    between = (blocks[:, None] < blocks[None, :]) & (blocks[None, :] < own_index)
    exponent = jnp.einsum(
        "cb,bh->ch", between.astype(jnp.float32), ends, precision=lax.Precision.HIGHEST
    )
    weight = jnp.where((blocks < own_index)[:, None], jnp.exp(exponent), 0.0)
    entering = jnp.einsum(
        "ch,chde->hde",
        weight,
        gathered[:, :, :head_width, :].astype(jnp.float32),
        precision=lax.Precision.HIGHEST,
    )
    state_low = entering.astype(jnp.bfloat16)
    token_ids = jnp.arange(row_count, dtype=jnp.int32)
    causal = token_ids[None, :] <= token_ids[:, None]
    log_gap = jnp.where(causal[None], cumul[:, :, None] - cumul[:, None, :], -jnp.inf)
    raw_scores = jnp.einsum("thd,shd->hts", queries, keys_here, preferred_element_type=jnp.float32)
    gated = (raw_scores * jnp.exp(log_gap)).astype(jnp.bfloat16)
    inner = jnp.einsum("hts,shd->thd", gated, vals_here, preferred_element_type=jnp.float32)
    outer = (
        jnp.einsum("thd,hde->the", queries, state_low, preferred_element_type=jnp.float32)
        * jnp.exp(cumul).T[:, :, None]
    )
    raw_out = inner + outer
    mean_sq = jnp.mean(raw_out * raw_out, axis=2, keepdims=True)
    normed = raw_out * lax.rsqrt(mean_sq + 1e-06) * norm_gain.reshape(heads_dev, head_width)[None]
    return normed.astype(jnp.bfloat16).reshape(row_count, heads_dev * head_width)


def to_heads(arrays, parts):
    rows, width = arrays[0].shape
    chunk = width // parts
    send = jnp.stack([a.reshape(rows, parts, chunk) for a in arrays], axis=1)
    send = send.transpose(2, 1, 0, 3)
    got = lax.all_to_all(send, "head", split_axis=0, concat_axis=0, tiled=True)
    return got.transpose(1, 0, 2, 3).reshape(len(arrays), parts * rows, chunk)


def to_tokens(arrays, parts):
    rows, chunk = arrays[0].shape
    send = jnp.stack([a.reshape(parts, rows // parts, chunk) for a in arrays], axis=1)
    got = lax.all_to_all(send, "head", split_axis=0, concat_axis=0, tiled=True)
    return got.transpose(1, 2, 0, 3).reshape(len(arrays), rows // parts, parts * chunk)


def per_device(
    q_soft, k_soft, v_soft, q_light, k_light, v_light, decay_log, norm_gain, doc_lengths
):
    parts = lax.axis_size("head")
    kv_soft = to_heads([k_soft, v_soft], parts)
    kv_soft, q_soft = lax.optimization_barrier((kv_soft, q_soft))
    rest = to_heads([q_soft, q_light, k_light, v_light], parts)
    heads_dev = decay_log.shape[0]
    row_count = kv_soft.shape[1]
    head_width = kv_soft.shape[2] // heads_dev
    light_out = lightning(
        rest[1], rest[2], rest[3], decay_log, norm_gain, row_count, heads_dev, head_width
    )
    soft_out = soft_attention(rest[0], kv_soft, doc_lengths, row_count, heads_dev, head_width)
    returned = to_tokens([soft_out, light_out], parts)
    return (returned[0], returned[1])


def solution(mesh):
    in_specs = (
        P(("ctx", "head"), None),
        P(("ctx", "head"), None),
        P(("ctx", "head"), None),
        P(("ctx", "head"), None),
        P(("ctx", "head"), None),
        P(("ctx", "head"), None),
        P("head", "ctx"),
        P("head"),
        P(),
    )
    out_specs = (P(("ctx", "head"), None), P(("ctx", "head"), None))
    return jax.shard_map(
        per_device, mesh=mesh, in_specs=in_specs, out_specs=out_specs, check_vma=False
    )
```

```python
from functools import partial

import jax
import jax.numpy as jnp
from jax import lax
from jax.sharding import PartitionSpec as P

DOC_REACH = 8


def shifted(block, axis, distance):
    size = lax.axis_size(axis)
    route = [(i, (i + distance) % size) for i in range(size)]
    return lax.ppermute(block, axis, route)


def doc_index(positions, starts):
    return jnp.sum((positions[:, None] >= starts[None, :]).astype(jnp.int32), axis=1) - 1


def block_partial(
    kv_pair,
    source,
    queries,
    query_pos,
    query_doc,
    starts,
    row_count,
    heads_dev,
    head_width,
):
    key_block = kv_pair[0].reshape(row_count, heads_dev, head_width)
    val_block = kv_pair[1].reshape(row_count, heads_dev, head_width)
    key_pos = source * row_count + jnp.arange(row_count, dtype=jnp.int32)
    key_doc = doc_index(key_pos, starts)
    allowed = (query_doc[:, None] == key_doc[None, :]) & (key_pos[None, :] <= query_pos[:, None])
    scores = (
        jnp.einsum("thd,shd->hts", queries, key_block, preferred_element_type=jnp.float32)
        / head_width**0.5
    )
    scores = jnp.where(allowed[None], scores, -1e30)
    block_max = jnp.max(scores, axis=2)
    probs = jnp.where(allowed[None], jnp.exp(scores - block_max[:, :, None]), 0.0)
    block_total = jnp.sum(probs, axis=2)
    product = jnp.einsum(
        "hts,shd->thd", probs.astype(jnp.bfloat16), val_block, preferred_element_type=jnp.float32
    )
    return (block_max, block_total, product)


def empty_partial(row_count, heads_dev, head_width):
    return (
        jnp.full((heads_dev, row_count), -1e30, jnp.float32),
        jnp.zeros((heads_dev, row_count), jnp.float32),
        jnp.zeros((row_count, heads_dev, head_width), jnp.float32),
    )


def soft_attention(q_rows, kv_pair, doc_lengths, row_count, heads_dev, head_width):
    size = lax.axis_size("ctx")
    own_index = lax.axis_index("ctx")
    reach = min(DOC_REACH, size - 1)
    forward_steps = (reach + 1) // 2
    starts = jnp.cumsum(doc_lengths) - doc_lengths
    query_pos = own_index * row_count + jnp.arange(row_count, dtype=jnp.int32)
    query_doc = doc_index(query_pos, starts)
    queries = q_rows.reshape(row_count, heads_dev, head_width)
    absorb = partial(
        block_partial,
        queries=queries,
        query_pos=query_pos,
        query_doc=query_doc,
        starts=starts,
        row_count=row_count,
        heads_dev=heads_dev,
        head_width=head_width,
    )
    skip = partial(empty_partial, row_count, heads_dev, head_width)

    def partial_of(block, offset):
        source = own_index - offset
        last_doc = doc_index(jnp.full((1,), source * row_count + row_count - 1, jnp.int32), starts)[
            0
        ]
        needed = (source >= 0) & (last_doc == query_doc[0])
        return lax.cond(needed, partial(absorb, block, source=source), skip)

    fwd_offsets = list(range(1, forward_steps + 1))
    bwd_offsets = list(range(reach, forward_steps, -1))
    partials = [absorb(kv_pair, source=own_index)]
    ahead = shifted(kv_pair, "ctx", 1)
    behind = shifted(kv_pair, "ctx", reach) if bwd_offsets else None
    for i in range(max(len(fwd_offsets), len(bwd_offsets))):
        now = []
        if i < len(fwd_offsets):
            now.append((ahead, fwd_offsets[i]))
        if i < len(bwd_offsets):
            now.append((behind, bwd_offsets[i]))
        ahead_next = shifted(ahead, "ctx", 1) if i + 1 < len(fwd_offsets) else None
        behind_next = shifted(behind, "ctx", -1) if i + 1 < len(bwd_offsets) else None
        done = [partial_of(block, offset) for block, offset in now]
        ahead_next, behind_next, done = lax.optimization_barrier((ahead_next, behind_next, done))
        partials.extend(done)
        ahead, behind = ahead_next, behind_next
    row_max = partials[0][0]
    for part in partials[1:]:
        row_max = jnp.maximum(row_max, part[0])
    run_total = jnp.zeros_like(row_max)
    run_acc = jnp.zeros_like(partials[0][2])
    for part in partials:
        scale = jnp.exp(part[0] - row_max)
        run_total = run_total + part[1] * scale
        run_acc = run_acc + part[2] * scale.T[:, :, None]
    mixed = run_acc / run_total.T[:, :, None]
    return mixed.astype(jnp.bfloat16).reshape(row_count, heads_dev * head_width)


def lightning(q_rows, k_rows, v_rows, decay_log, norm_gain, row_count, heads_dev, head_width):
    size = lax.axis_size("ctx")
    own_index = lax.axis_index("ctx")
    cumul = jnp.cumsum(decay_log, axis=1)
    block_end = cumul[:, -1:]
    queries = q_rows.reshape(row_count, heads_dev, head_width)
    keys_here = k_rows.reshape(row_count, heads_dev, head_width)
    vals_here = v_rows.reshape(row_count, heads_dev, head_width)
    weighted = (keys_here * jnp.exp(block_end - cumul).T[:, :, None]).astype(jnp.bfloat16)
    update = jnp.einsum("thd,the->hde", weighted, vals_here, preferred_element_type=jnp.float32)
    end_hi = block_end.astype(jnp.bfloat16)
    end_lo = (block_end - end_hi.astype(jnp.float32)).astype(jnp.bfloat16)
    extra = jnp.zeros((heads_dev, 16, head_width), jnp.bfloat16)
    extra = extra.at[:, 0, :].set(jnp.broadcast_to(end_hi, (heads_dev, head_width)))
    extra = extra.at[:, 1, :].set(jnp.broadcast_to(end_lo, (heads_dev, head_width)))
    packed = jnp.concatenate([update.astype(jnp.bfloat16), extra], axis=1)
    gathered = lax.all_gather(packed, "ctx")
    ends = gathered[:, :, head_width, 0].astype(jnp.float32) + gathered[
        :, :, head_width + 1, 0
    ].astype(jnp.float32)
    blocks = jnp.arange(size, dtype=jnp.int32)
    between = (blocks[:, None] < blocks[None, :]) & (blocks[None, :] < own_index)
    exponent = jnp.einsum(
        "cb,bh->ch", between.astype(jnp.float32), ends, precision=lax.Precision.HIGHEST
    )
    weight = jnp.where((blocks < own_index)[:, None], jnp.exp(exponent), 0.0)
    entering = jnp.einsum(
        "ch,chde->hde",
        weight,
        gathered[:, :, :head_width, :].astype(jnp.float32),
        precision=lax.Precision.HIGHEST,
    )
    state_low = entering.astype(jnp.bfloat16)
    token_ids = jnp.arange(row_count, dtype=jnp.int32)
    causal = token_ids[None, :] <= token_ids[:, None]
    log_gap = jnp.where(causal[None], cumul[:, :, None] - cumul[:, None, :], -jnp.inf)
    raw_scores = jnp.einsum("thd,shd->hts", queries, keys_here, preferred_element_type=jnp.float32)
    gated = (raw_scores * jnp.exp(log_gap)).astype(jnp.bfloat16)
    inner = jnp.einsum("hts,shd->thd", gated, vals_here, preferred_element_type=jnp.float32)
    outer = (
        jnp.einsum("thd,hde->the", queries, state_low, preferred_element_type=jnp.float32)
        * jnp.exp(cumul).T[:, :, None]
    )
    raw_out = inner + outer
    mean_sq = jnp.mean(raw_out * raw_out, axis=2, keepdims=True)
    normed = raw_out * lax.rsqrt(mean_sq + 1e-06) * norm_gain.reshape(heads_dev, head_width)[None]
    return normed.astype(jnp.bfloat16).reshape(row_count, heads_dev * head_width)


def to_heads(arrays, parts):
    rows, width = arrays[0].shape
    chunk = width // parts
    send = jnp.stack([a.reshape(rows, parts, chunk) for a in arrays], axis=1)
    send = send.transpose(2, 1, 0, 3)
    got = lax.all_to_all(send, "head", split_axis=0, concat_axis=0, tiled=True)
    return got.transpose(1, 0, 2, 3).reshape(len(arrays), parts * rows, chunk)


def to_tokens(arrays, parts):
    rows, chunk = arrays[0].shape
    send = jnp.stack([a.reshape(parts, rows // parts, chunk) for a in arrays], axis=1)
    got = lax.all_to_all(send, "head", split_axis=0, concat_axis=0, tiled=True)
    return got.transpose(1, 2, 0, 3).reshape(len(arrays), rows // parts, parts * chunk)


def per_device(
    q_soft, k_soft, v_soft, q_light, k_light, v_light, decay_log, norm_gain, doc_lengths
):
    parts = lax.axis_size("head")
    moved = to_heads([k_soft, v_soft, q_soft, q_light, k_light, v_light], parts)
    kv_soft = moved[:2]
    rest = moved[2:]
    heads_dev = decay_log.shape[0]
    row_count = kv_soft.shape[1]
    head_width = kv_soft.shape[2] // heads_dev
    light_out = lightning(
        rest[1], rest[2], rest[3], decay_log, norm_gain, row_count, heads_dev, head_width
    )
    soft_out = soft_attention(rest[0], kv_soft, doc_lengths, row_count, heads_dev, head_width)
    returned = to_tokens([soft_out, light_out], parts)
    return (returned[0], returned[1])


def solution(mesh):
    in_specs = (
        P(("ctx", "head"), None),
        P(("ctx", "head"), None),
        P(("ctx", "head"), None),
        P(("ctx", "head"), None),
        P(("ctx", "head"), None),
        P(("ctx", "head"), None),
        P("head", "ctx"),
        P("head"),
        P(),
    )
    out_specs = (P(("ctx", "head"), None), P(("ctx", "head"), None))
    return jax.shard_map(
        per_device, mesh=mesh, in_specs=in_specs, out_specs=out_specs, check_vma=False
    )
```

```python
from functools import partial

import jax
import jax.numpy as jnp
from jax import lax
from jax.experimental import pallas as pl
from jax.sharding import PartitionSpec as P

DOC_REACH = 8


def shifted(block, axis, distance):
    size = lax.axis_size(axis)
    route = [(i, (i + distance) % size) for i in range(size)]
    return lax.ppermute(block, axis, route)


def doc_index(positions, starts):
    return jnp.sum((positions[:, None] >= starts[None, :]).astype(jnp.int32), axis=1) - 1


def online_block_kernel(
    q_doc, k_doc, q_pos, k_pos, q_ref, k_ref, v_ref, m_in, l_in, acc_in, m_out, l_out, acc_out
):
    heads_dev = m_in.shape[0]
    head_width = q_ref.shape[1] // heads_dev
    allowed = (q_doc[...] == k_doc[...]) & (k_pos[...] <= q_pos[...])
    for h in range(heads_dev):
        cols = slice(h * head_width, (h + 1) * head_width)
        scores = lax.dot_general(
            q_ref[:, cols],
            k_ref[:, cols],
            (((1,), (1,)), ((), ())),
            preferred_element_type=jnp.float32,
        )
        scores = jnp.where(allowed, scores / head_width**0.5, -1e30)
        run_max = m_in[h][:, :1]
        new_max = jnp.maximum(run_max, jnp.max(scores, axis=1, keepdims=True))
        correction = jnp.exp(run_max - new_max)
        probs = jnp.where(allowed, jnp.exp(scores - new_max), 0.0)
        new_total = l_in[h][:, :1] * correction + jnp.sum(probs, axis=1, keepdims=True)
        product = jnp.dot(
            probs.astype(jnp.bfloat16), v_ref[:, cols], preferred_element_type=jnp.float32
        )
        acc_out[:, cols] = acc_in[:, cols] * correction + product
        m_out[h] = jnp.broadcast_to(new_max, m_out.shape[1:])
        l_out[h] = jnp.broadcast_to(new_total, l_out.shape[1:])


def online_block(running, kv_pair, queries, query_doc, query_pos, key_doc, key_pos):
    run_max, run_total, run_acc = running
    rows, width = queries.shape
    heads_dev = run_max.shape[0]
    flops = 4 * rows * rows * width
    return pl.pallas_call(
        online_block_kernel,
        out_shape=(
            jax.ShapeDtypeStruct(run_max.shape, jnp.float32),
            jax.ShapeDtypeStruct(run_total.shape, jnp.float32),
            jax.ShapeDtypeStruct(run_acc.shape, jnp.float32),
        ),
        input_output_aliases={7: 0, 8: 1, 9: 2},
        cost_estimate=pl.CostEstimate(
            flops=flops, transcendentals=heads_dev * rows * rows, bytes_accessed=6 * rows * width * 4
        ),
    )(
        query_doc[:, None],
        key_doc[None, :],
        query_pos[:, None],
        key_pos[None, :],
        queries,
        kv_pair[0],
        kv_pair[1],
        run_max,
        run_total,
        run_acc,
    )


def soft_attention(q_rows, kv_pair, doc_lengths, row_count, heads_dev, head_width):
    size = lax.axis_size("ctx")
    own_index = lax.axis_index("ctx")
    reach = min(DOC_REACH, size - 1)
    forward_steps = (reach + 1) // 2
    starts = jnp.cumsum(doc_lengths) - doc_lengths
    query_pos = own_index * row_count + jnp.arange(row_count, dtype=jnp.int32)
    query_doc = doc_index(query_pos, starts)
    lanes = 128
    running = (
        jnp.full((heads_dev, row_count, lanes), -1e30, jnp.float32),
        jnp.zeros((heads_dev, row_count, lanes), jnp.float32),
        jnp.zeros((row_count, heads_dev * head_width), jnp.float32),
    )

    def absorb(running, block, source):
        key_pos = source * row_count + jnp.arange(row_count, dtype=jnp.int32)
        key_doc = doc_index(key_pos, starts)
        return online_block(running, block, q_rows, query_doc, query_pos, key_doc, key_pos)

    def absorb_if_needed(running, block, offset):
        source = own_index - offset
        last_doc = doc_index(jnp.full((1,), source * row_count + row_count - 1, jnp.int32), starts)[
            0
        ]
        needed = (source >= 0) & (last_doc == query_doc[0])
        return lax.cond(
            needed, lambda r: absorb(r, block, source), lambda r: r, running
        )

    fwd_offsets = list(range(1, forward_steps + 1))
    bwd_offsets = list(range(reach, forward_steps, -1))
    running = absorb(running, kv_pair, own_index)
    ahead = shifted(kv_pair, "ctx", 1)
    behind = shifted(kv_pair, "ctx", reach) if bwd_offsets else None
    for i in range(max(len(fwd_offsets), len(bwd_offsets))):
        ahead_next = shifted(ahead, "ctx", 1) if i + 1 < len(fwd_offsets) else None
        behind_next = shifted(behind, "ctx", -1) if i + 1 < len(bwd_offsets) else None
        if i < len(fwd_offsets):
            running = absorb_if_needed(running, ahead, fwd_offsets[i])
        if i < len(bwd_offsets):
            running = absorb_if_needed(running, behind, bwd_offsets[i])
        ahead_next, behind_next, running = lax.optimization_barrier(
            (ahead_next, behind_next, running)
        )
        ahead, behind = ahead_next, behind_next
    run_max, run_total, run_acc = running
    totals = run_total[:, :, 0].T
    mixed = run_acc.reshape(row_count, heads_dev, head_width) / totals[:, :, None]
    return mixed.astype(jnp.bfloat16).reshape(row_count, heads_dev * head_width)


def lightning(q_rows, k_rows, v_rows, decay_log, norm_gain, row_count, heads_dev, head_width):
    size = lax.axis_size("ctx")
    own_index = lax.axis_index("ctx")
    cumul = jnp.cumsum(decay_log, axis=1)
    block_end = cumul[:, -1:]
    queries = q_rows.reshape(row_count, heads_dev, head_width)
    keys_here = k_rows.reshape(row_count, heads_dev, head_width)
    vals_here = v_rows.reshape(row_count, heads_dev, head_width)
    weighted = (keys_here * jnp.exp(block_end - cumul).T[:, :, None]).astype(jnp.bfloat16)
    update = jnp.einsum("thd,the->hde", weighted, vals_here, preferred_element_type=jnp.float32)
    end_hi = block_end.astype(jnp.bfloat16)
    end_lo = (block_end - end_hi.astype(jnp.float32)).astype(jnp.bfloat16)
    extra = jnp.zeros((heads_dev, 16, head_width), jnp.bfloat16)
    extra = extra.at[:, 0, :].set(jnp.broadcast_to(end_hi, (heads_dev, head_width)))
    extra = extra.at[:, 1, :].set(jnp.broadcast_to(end_lo, (heads_dev, head_width)))
    packed = jnp.concatenate([update.astype(jnp.bfloat16), extra], axis=1)
    gathered = lax.all_gather(packed, "ctx")
    ends = gathered[:, :, head_width, 0].astype(jnp.float32) + gathered[
        :, :, head_width + 1, 0
    ].astype(jnp.float32)
    blocks = jnp.arange(size, dtype=jnp.int32)
    between = (blocks[:, None] < blocks[None, :]) & (blocks[None, :] < own_index)
    exponent = jnp.einsum(
        "cb,bh->ch", between.astype(jnp.float32), ends, precision=lax.Precision.HIGHEST
    )
    weight = jnp.where((blocks < own_index)[:, None], jnp.exp(exponent), 0.0)
    entering = jnp.einsum(
        "ch,chde->hde",
        weight,
        gathered[:, :, :head_width, :].astype(jnp.float32),
        precision=lax.Precision.HIGHEST,
    )
    state_low = entering.astype(jnp.bfloat16)
    token_ids = jnp.arange(row_count, dtype=jnp.int32)
    causal = token_ids[None, :] <= token_ids[:, None]
    log_gap = jnp.where(causal[None], cumul[:, :, None] - cumul[:, None, :], -jnp.inf)
    raw_scores = jnp.einsum("thd,shd->hts", queries, keys_here, preferred_element_type=jnp.float32)
    gated = (raw_scores * jnp.exp(log_gap)).astype(jnp.bfloat16)
    inner = jnp.einsum("hts,shd->thd", gated, vals_here, preferred_element_type=jnp.float32)
    outer = (
        jnp.einsum("thd,hde->the", queries, state_low, preferred_element_type=jnp.float32)
        * jnp.exp(cumul).T[:, :, None]
    )
    raw_out = inner + outer
    mean_sq = jnp.mean(raw_out * raw_out, axis=2, keepdims=True)
    normed = raw_out * lax.rsqrt(mean_sq + 1e-06) * norm_gain.reshape(heads_dev, head_width)[None]
    return normed.astype(jnp.bfloat16).reshape(row_count, heads_dev * head_width)


def to_heads(arrays, parts):
    rows, width = arrays[0].shape
    chunk = width // parts
    send = jnp.stack([a.reshape(rows, parts, chunk) for a in arrays], axis=1)
    send = send.transpose(2, 1, 0, 3)
    got = lax.all_to_all(send, "head", split_axis=0, concat_axis=0, tiled=True)
    return got.transpose(1, 0, 2, 3).reshape(len(arrays), parts * rows, chunk)


def to_tokens(arrays, parts):
    rows, chunk = arrays[0].shape
    send = jnp.stack([a.reshape(parts, rows // parts, chunk) for a in arrays], axis=1)
    got = lax.all_to_all(send, "head", split_axis=0, concat_axis=0, tiled=True)
    return got.transpose(1, 2, 0, 3).reshape(len(arrays), rows // parts, parts * chunk)


def per_device(
    q_soft, k_soft, v_soft, q_light, k_light, v_light, decay_log, norm_gain, doc_lengths
):
    parts = lax.axis_size("head")
    moved = to_heads([k_soft, v_soft, q_soft, q_light, k_light, v_light], parts)
    kv_soft = moved[:2]
    rest = moved[2:]
    heads_dev = decay_log.shape[0]
    row_count = kv_soft.shape[1]
    head_width = kv_soft.shape[2] // heads_dev
    light_out = lightning(
        rest[1], rest[2], rest[3], decay_log, norm_gain, row_count, heads_dev, head_width
    )
    soft_out = soft_attention(rest[0], kv_soft, doc_lengths, row_count, heads_dev, head_width)
    returned = to_tokens([soft_out, light_out], parts)
    return (returned[0], returned[1])


def solution(mesh):
    in_specs = (
        P(("ctx", "head"), None),
        P(("ctx", "head"), None),
        P(("ctx", "head"), None),
        P(("ctx", "head"), None),
        P(("ctx", "head"), None),
        P(("ctx", "head"), None),
        P("head", "ctx"),
        P("head"),
        P(),
    )
    out_specs = (P(("ctx", "head"), None), P(("ctx", "head"), None))
    return jax.shard_map(
        per_device, mesh=mesh, in_specs=in_specs, out_specs=out_specs, check_vma=False
    )
```

```python
from functools import partial

import jax
import jax.numpy as jnp
from jax import lax
from jax.experimental import pallas as pl
from jax.sharding import PartitionSpec as P

DOC_REACH = 8


def shifted(block, axis, distance):
    size = lax.axis_size(axis)
    route = [(i, (i + distance) % size) for i in range(size)]
    return lax.ppermute(block, axis, route)


def doc_index(positions, starts):
    return jnp.sum((positions[:, None] >= starts[None, :]).astype(jnp.int32), axis=1) - 1


def online_block_kernel(
    q_doc, k_doc, q_pos, k_pos, q_ref, kv_ref, m_in, l_in, acc_in, m_out, l_out, acc_out
):
    heads_dev = m_in.shape[0]
    head_width = q_ref.shape[1] // heads_dev
    k_ref = kv_ref.at[0]
    v_ref = kv_ref.at[1]
    allowed = (q_doc[:, :1] == k_doc[:1, :]) & (k_pos[:1, :] <= q_pos[:, :1])
    for h in range(heads_dev):
        cols = slice(h * head_width, (h + 1) * head_width)
        scores = lax.dot_general(
            q_ref[:, cols],
            k_ref[:, cols],
            (((1,), (1,)), ((), ())),
            preferred_element_type=jnp.float32,
        )
        scores = jnp.where(allowed, scores * (1.0 / head_width**0.5), -1e30)
        run_max = m_in[h][:, :1]
        new_max = jnp.maximum(run_max, jnp.max(scores, axis=1, keepdims=True))
        correction = jnp.exp(run_max - new_max)
        probs = jnp.where(allowed, jnp.exp(scores - new_max), 0.0)
        new_total = l_in[h][:, :1] * correction + jnp.sum(probs, axis=1, keepdims=True)
        product = jnp.dot(
            probs.astype(jnp.bfloat16), v_ref[:, cols], preferred_element_type=jnp.float32
        )
        acc_out[:, cols] = acc_in[:, cols] * correction + product
        m_out[h] = jnp.broadcast_to(new_max, m_out.shape[1:])
        l_out[h] = jnp.broadcast_to(new_total, l_out.shape[1:])


def online_block(running, kv_pair, queries, query_doc, query_pos, key_doc, key_pos):
    run_max, run_total, run_acc = running
    rows, width = queries.shape
    heads_dev = run_max.shape[0]
    flops = 4 * rows * rows * width
    return pl.pallas_call(
        online_block_kernel,
        out_shape=(
            jax.ShapeDtypeStruct(run_max.shape, jnp.float32),
            jax.ShapeDtypeStruct(run_total.shape, jnp.float32),
            jax.ShapeDtypeStruct(run_acc.shape, jnp.float32),
        ),
        input_output_aliases={6: 0, 7: 1, 8: 2},
        cost_estimate=pl.CostEstimate(
            flops=flops, transcendentals=heads_dev * rows * rows, bytes_accessed=6 * rows * width * 4
        ),
    )(
        query_doc,
        key_doc,
        query_pos,
        key_pos,
        queries,
        kv_pair,
        run_max,
        run_total,
        run_acc,
    )


def soft_attention(q_rows, kv_pair, doc_lengths, row_count, heads_dev, head_width):
    size = lax.axis_size("ctx")
    own_index = lax.axis_index("ctx")
    reach = min(DOC_REACH, size - 1)
    forward_steps = (reach + 1) // 2
    starts = jnp.cumsum(doc_lengths) - doc_lengths
    query_pos = own_index * row_count + jnp.arange(row_count, dtype=jnp.int32)
    query_doc = doc_index(query_pos, starts)
    lanes = 128
    query_doc_wide = jnp.broadcast_to(query_doc[:, None], (row_count, lanes))
    query_pos_wide = jnp.broadcast_to(query_pos[:, None], (row_count, lanes))
    running = (
        jnp.full((heads_dev, row_count, lanes), -1e30, jnp.float32),
        jnp.zeros((heads_dev, row_count, lanes), jnp.float32),
        jnp.zeros((row_count, heads_dev * head_width), jnp.float32),
    )

    def absorb(running, block, source):
        key_pos = source * row_count + jnp.arange(row_count, dtype=jnp.int32)
        key_doc = doc_index(key_pos, starts)
        return online_block(
            running,
            block,
            q_rows,
            query_doc_wide,
            query_pos_wide,
            jnp.broadcast_to(key_doc[None, :], (8, row_count)),
            jnp.broadcast_to(key_pos[None, :], (8, row_count)),
        )

    def absorb_if_needed(running, block, offset):
        source = own_index - offset
        last_doc = doc_index(jnp.full((1,), source * row_count + row_count - 1, jnp.int32), starts)[
            0
        ]
        needed = (source >= 0) & (last_doc == query_doc[0])
        return lax.cond(
            needed, lambda r: absorb(r, block, source), lambda r: r, running
        )

    fwd_offsets = list(range(1, forward_steps + 1))
    bwd_offsets = list(range(reach, forward_steps, -1))
    running = absorb(running, kv_pair, own_index)
    ahead = shifted(kv_pair, "ctx", 1)
    behind = shifted(kv_pair, "ctx", reach) if bwd_offsets else None
    for i in range(max(len(fwd_offsets), len(bwd_offsets))):
        ahead_next = shifted(ahead, "ctx", 1) if i + 1 < len(fwd_offsets) else None
        behind_next = shifted(behind, "ctx", -1) if i + 1 < len(bwd_offsets) else None
        if i < len(fwd_offsets):
            running = absorb_if_needed(running, ahead, fwd_offsets[i])
        if i < len(bwd_offsets):
            running = absorb_if_needed(running, behind, bwd_offsets[i])
        ahead_next, behind_next, running = lax.optimization_barrier(
            (ahead_next, behind_next, running)
        )
        ahead, behind = ahead_next, behind_next
    run_max, run_total, run_acc = running
    totals = run_total[:, :, 0].T
    mixed = run_acc.reshape(row_count, heads_dev, head_width) / totals[:, :, None]
    return mixed.astype(jnp.bfloat16).reshape(row_count, heads_dev * head_width)


def lightning(q_rows, k_rows, v_rows, decay_log, norm_gain, row_count, heads_dev, head_width):
    size = lax.axis_size("ctx")
    own_index = lax.axis_index("ctx")
    cumul = jnp.cumsum(decay_log, axis=1)
    block_end = cumul[:, -1:]
    queries = q_rows.reshape(row_count, heads_dev, head_width)
    keys_here = k_rows.reshape(row_count, heads_dev, head_width)
    vals_here = v_rows.reshape(row_count, heads_dev, head_width)
    weighted = (keys_here * jnp.exp(block_end - cumul).T[:, :, None]).astype(jnp.bfloat16)
    update = jnp.einsum("thd,the->hde", weighted, vals_here, preferred_element_type=jnp.float32)
    end_hi = block_end.astype(jnp.bfloat16)
    end_lo = (block_end - end_hi.astype(jnp.float32)).astype(jnp.bfloat16)
    extra = jnp.zeros((heads_dev, 16, head_width), jnp.bfloat16)
    extra = extra.at[:, 0, :].set(jnp.broadcast_to(end_hi, (heads_dev, head_width)))
    extra = extra.at[:, 1, :].set(jnp.broadcast_to(end_lo, (heads_dev, head_width)))
    packed = jnp.concatenate([update.astype(jnp.bfloat16), extra], axis=1)
    gathered = lax.all_gather(packed, "ctx")
    ends = gathered[:, :, head_width, 0].astype(jnp.float32) + gathered[
        :, :, head_width + 1, 0
    ].astype(jnp.float32)
    blocks = jnp.arange(size, dtype=jnp.int32)
    between = (blocks[:, None] < blocks[None, :]) & (blocks[None, :] < own_index)
    exponent = jnp.einsum(
        "cb,bh->ch", between.astype(jnp.float32), ends, precision=lax.Precision.HIGHEST
    )
    weight = jnp.where((blocks < own_index)[:, None], jnp.exp(exponent), 0.0)
    entering = jnp.einsum(
        "ch,chde->hde",
        weight,
        gathered[:, :, :head_width, :].astype(jnp.float32),
        precision=lax.Precision.HIGHEST,
    )
    state_low = entering.astype(jnp.bfloat16)
    token_ids = jnp.arange(row_count, dtype=jnp.int32)
    causal = token_ids[None, :] <= token_ids[:, None]
    log_gap = jnp.where(causal[None], cumul[:, :, None] - cumul[:, None, :], -jnp.inf)
    raw_scores = jnp.einsum("thd,shd->hts", queries, keys_here, preferred_element_type=jnp.float32)
    gated = (raw_scores * jnp.exp(log_gap)).astype(jnp.bfloat16)
    inner = jnp.einsum("hts,shd->thd", gated, vals_here, preferred_element_type=jnp.float32)
    outer = (
        jnp.einsum("thd,hde->the", queries, state_low, preferred_element_type=jnp.float32)
        * jnp.exp(cumul).T[:, :, None]
    )
    raw_out = inner + outer
    mean_sq = jnp.mean(raw_out * raw_out, axis=2, keepdims=True)
    normed = raw_out * lax.rsqrt(mean_sq + 1e-06) * norm_gain.reshape(heads_dev, head_width)[None]
    return normed.astype(jnp.bfloat16).reshape(row_count, heads_dev * head_width)


def to_heads(arrays, parts):
    rows, width = arrays[0].shape
    chunk = width // parts
    send = jnp.stack([a.reshape(rows, parts, chunk) for a in arrays], axis=1)
    send = send.transpose(2, 1, 0, 3)
    got = lax.all_to_all(send, "head", split_axis=0, concat_axis=0, tiled=True)
    return got.transpose(1, 0, 2, 3).reshape(len(arrays), parts * rows, chunk)


def to_tokens(arrays, parts):
    rows, chunk = arrays[0].shape
    send = jnp.stack([a.reshape(parts, rows // parts, chunk) for a in arrays], axis=1)
    got = lax.all_to_all(send, "head", split_axis=0, concat_axis=0, tiled=True)
    return got.transpose(1, 2, 0, 3).reshape(len(arrays), rows // parts, parts * chunk)


def per_device(
    q_soft, k_soft, v_soft, q_light, k_light, v_light, decay_log, norm_gain, doc_lengths
):
    parts = lax.axis_size("head")
    moved = to_heads([k_soft, v_soft, q_soft, q_light, k_light, v_light], parts)
    kv_soft = moved[:2]
    rest = moved[2:]
    heads_dev = decay_log.shape[0]
    row_count = kv_soft.shape[1]
    head_width = kv_soft.shape[2] // heads_dev
    light_out = lightning(
        rest[1], rest[2], rest[3], decay_log, norm_gain, row_count, heads_dev, head_width
    )
    soft_out = soft_attention(rest[0], kv_soft, doc_lengths, row_count, heads_dev, head_width)
    returned = to_tokens([soft_out, light_out], parts)
    return (returned[0], returned[1])


def solution(mesh):
    in_specs = (
        P(("ctx", "head"), None),
        P(("ctx", "head"), None),
        P(("ctx", "head"), None),
        P(("ctx", "head"), None),
        P(("ctx", "head"), None),
        P(("ctx", "head"), None),
        P("head", "ctx"),
        P("head"),
        P(),
    )
    out_specs = (P(("ctx", "head"), None), P(("ctx", "head"), None))
    return jax.shard_map(
        per_device, mesh=mesh, in_specs=in_specs, out_specs=out_specs, check_vma=False
    )
```

```python
from functools import partial

import jax
import jax.numpy as jnp
from jax import lax
from jax.experimental import pallas as pl
from jax.sharding import PartitionSpec as P

DOC_REACH = 8


def shifted(block, axis, distance):
    size = lax.axis_size(axis)
    route = [(i, (i + distance) % size) for i in range(size)]
    return lax.ppermute(block, axis, route)


def doc_index(positions, starts):
    return jnp.sum((positions[:, None] >= starts[None, :]).astype(jnp.int32), axis=1) - 1


def online_block_kernel(
    q_doc, k_doc, q_pos, k_pos, q_ref, kv_ref, m_in, l_in, acc_in, m_out, l_out, acc_out
):
    heads_dev = m_in.shape[0]
    rows = q_ref.shape[0]
    head_width = q_ref.shape[1] // heads_dev
    chunk = 128
    key_doc = k_doc[:1, :]
    key_pos = k_pos[:1, :]

    def body(i, carry):
        r = pl.ds(pl.multiple_of(i * chunk, chunk), chunk)
        allowed = (q_doc[r, :1] == key_doc) & (key_pos <= q_pos[r, :1])
        for h in range(heads_dev):
            cols = slice(h * head_width, (h + 1) * head_width)
            scores = lax.dot_general(
                q_ref[r, cols],
                kv_ref[0, :, cols],
                (((1,), (1,)), ((), ())),
                preferred_element_type=jnp.float32,
            )
            scores = jnp.where(allowed, scores * (1.0 / head_width**0.5), -1e30)
            run_max = m_in[h, r, :1]
            new_max = jnp.maximum(run_max, jnp.max(scores, axis=1, keepdims=True))
            correction = jnp.exp(run_max - new_max)
            probs = jnp.exp(scores - new_max)
            new_total = l_in[h, r, :1] * correction + jnp.sum(probs, axis=1, keepdims=True)
            product = jnp.dot(
                probs.astype(jnp.bfloat16), kv_ref[1, :, cols], preferred_element_type=jnp.float32
            )
            acc_out[r, cols] = acc_in[r, cols] * correction + product
            m_out[h, r, :] = jnp.broadcast_to(new_max, (chunk, m_out.shape[2]))
            l_out[h, r, :] = jnp.broadcast_to(new_total, (chunk, l_out.shape[2]))
        return carry

    lax.fori_loop(0, rows // chunk, body, 0)


def online_block(running, kv_pair, queries, query_doc, query_pos, key_doc, key_pos):
    run_max, run_total, run_acc = running
    rows, width = queries.shape
    heads_dev = run_max.shape[0]
    flops = 4 * rows * rows * width
    return pl.pallas_call(
        online_block_kernel,
        out_shape=(
            jax.ShapeDtypeStruct(run_max.shape, jnp.float32),
            jax.ShapeDtypeStruct(run_total.shape, jnp.float32),
            jax.ShapeDtypeStruct(run_acc.shape, jnp.float32),
        ),
        input_output_aliases={6: 0, 7: 1, 8: 2},
        cost_estimate=pl.CostEstimate(
            flops=flops, transcendentals=heads_dev * rows * rows, bytes_accessed=6 * rows * width * 4
        ),
    )(
        query_doc,
        key_doc,
        query_pos,
        key_pos,
        queries,
        kv_pair,
        run_max,
        run_total,
        run_acc,
    )


def soft_attention(q_rows, kv_pair, doc_lengths, row_count, heads_dev, head_width):
    size = lax.axis_size("ctx")
    own_index = lax.axis_index("ctx")
    reach = min(DOC_REACH, size - 1)
    forward_steps = (reach + 1) // 2
    starts = jnp.cumsum(doc_lengths) - doc_lengths
    query_pos = own_index * row_count + jnp.arange(row_count, dtype=jnp.int32)
    query_doc = doc_index(query_pos, starts)
    lanes = 128
    query_doc_wide = jnp.broadcast_to(query_doc[:, None], (row_count, lanes))
    query_pos_wide = jnp.broadcast_to(query_pos[:, None], (row_count, lanes))
    running = (
        jnp.full((heads_dev, row_count, lanes), -1e30, jnp.float32),
        jnp.zeros((heads_dev, row_count, lanes), jnp.float32),
        jnp.zeros((row_count, heads_dev * head_width), jnp.float32),
    )

    def absorb(running, block, source):
        key_pos = source * row_count + jnp.arange(row_count, dtype=jnp.int32)
        key_doc = doc_index(key_pos, starts)
        return online_block(
            running,
            block,
            q_rows,
            query_doc_wide,
            query_pos_wide,
            jnp.broadcast_to(key_doc[None, :], (8, row_count)),
            jnp.broadcast_to(key_pos[None, :], (8, row_count)),
        )

    def absorb_if_needed(running, block, offset):
        source = own_index - offset
        last_doc = doc_index(jnp.full((1,), source * row_count + row_count - 1, jnp.int32), starts)[
            0
        ]
        needed = (source >= 0) & (last_doc == query_doc[0])
        return lax.cond(
            needed, lambda r: absorb(r, block, source), lambda r: r, running
        )

    fwd_offsets = list(range(1, forward_steps + 1))
    bwd_offsets = list(range(reach, forward_steps, -1))
    running = absorb(running, kv_pair, own_index)
    ahead = shifted(kv_pair, "ctx", 1)
    behind = shifted(kv_pair, "ctx", reach) if bwd_offsets else None
    for i in range(max(len(fwd_offsets), len(bwd_offsets))):
        ahead_next = shifted(ahead, "ctx", 1) if i + 1 < len(fwd_offsets) else None
        behind_next = shifted(behind, "ctx", -1) if i + 1 < len(bwd_offsets) else None
        if i < len(fwd_offsets):
            running = absorb_if_needed(running, ahead, fwd_offsets[i])
        if i < len(bwd_offsets):
            running = absorb_if_needed(running, behind, bwd_offsets[i])
        ahead_next, behind_next, running = lax.optimization_barrier(
            (ahead_next, behind_next, running)
        )
        ahead, behind = ahead_next, behind_next
    run_max, run_total, run_acc = running
    totals = run_total[:, :, 0].T
    mixed = run_acc.reshape(row_count, heads_dev, head_width) / totals[:, :, None]
    return mixed.astype(jnp.bfloat16).reshape(row_count, heads_dev * head_width)


def lightning(q_rows, k_rows, v_rows, decay_log, norm_gain, row_count, heads_dev, head_width):
    size = lax.axis_size("ctx")
    own_index = lax.axis_index("ctx")
    cumul = jnp.cumsum(decay_log, axis=1)
    block_end = cumul[:, -1:]
    queries = q_rows.reshape(row_count, heads_dev, head_width)
    keys_here = k_rows.reshape(row_count, heads_dev, head_width)
    vals_here = v_rows.reshape(row_count, heads_dev, head_width)
    weighted = (keys_here * jnp.exp(block_end - cumul).T[:, :, None]).astype(jnp.bfloat16)
    update = jnp.einsum("thd,the->hde", weighted, vals_here, preferred_element_type=jnp.float32)
    end_hi = block_end.astype(jnp.bfloat16)
    end_lo = (block_end - end_hi.astype(jnp.float32)).astype(jnp.bfloat16)
    extra = jnp.zeros((heads_dev, 16, head_width), jnp.bfloat16)
    extra = extra.at[:, 0, :].set(jnp.broadcast_to(end_hi, (heads_dev, head_width)))
    extra = extra.at[:, 1, :].set(jnp.broadcast_to(end_lo, (heads_dev, head_width)))
    packed = jnp.concatenate([update.astype(jnp.bfloat16), extra], axis=1)
    gathered = lax.all_gather(packed, "ctx")
    ends = gathered[:, :, head_width, 0].astype(jnp.float32) + gathered[
        :, :, head_width + 1, 0
    ].astype(jnp.float32)
    blocks = jnp.arange(size, dtype=jnp.int32)
    between = (blocks[:, None] < blocks[None, :]) & (blocks[None, :] < own_index)
    exponent = jnp.einsum(
        "cb,bh->ch", between.astype(jnp.float32), ends, precision=lax.Precision.HIGHEST
    )
    weight = jnp.where((blocks < own_index)[:, None], jnp.exp(exponent), 0.0)
    entering = jnp.einsum(
        "ch,chde->hde",
        weight,
        gathered[:, :, :head_width, :].astype(jnp.float32),
        precision=lax.Precision.HIGHEST,
    )
    state_low = entering.astype(jnp.bfloat16)
    token_ids = jnp.arange(row_count, dtype=jnp.int32)
    causal = token_ids[None, :] <= token_ids[:, None]
    log_gap = jnp.where(causal[None], cumul[:, :, None] - cumul[:, None, :], -jnp.inf)
    raw_scores = jnp.einsum("thd,shd->hts", queries, keys_here, preferred_element_type=jnp.float32)
    gated = (raw_scores * jnp.exp(log_gap)).astype(jnp.bfloat16)
    inner = jnp.einsum("hts,shd->thd", gated, vals_here, preferred_element_type=jnp.float32)
    outer = (
        jnp.einsum("thd,hde->the", queries, state_low, preferred_element_type=jnp.float32)
        * jnp.exp(cumul).T[:, :, None]
    )
    raw_out = inner + outer
    mean_sq = jnp.mean(raw_out * raw_out, axis=2, keepdims=True)
    normed = raw_out * lax.rsqrt(mean_sq + 1e-06) * norm_gain.reshape(heads_dev, head_width)[None]
    return normed.astype(jnp.bfloat16).reshape(row_count, heads_dev * head_width)


def to_heads(arrays, parts):
    rows, width = arrays[0].shape
    chunk = width // parts
    send = jnp.stack([a.reshape(rows, parts, chunk) for a in arrays], axis=1)
    send = send.transpose(2, 1, 0, 3)
    got = lax.all_to_all(send, "head", split_axis=0, concat_axis=0, tiled=True)
    return got.transpose(1, 0, 2, 3).reshape(len(arrays), parts * rows, chunk)


def to_tokens(arrays, parts):
    rows, chunk = arrays[0].shape
    send = jnp.stack([a.reshape(parts, rows // parts, chunk) for a in arrays], axis=1)
    got = lax.all_to_all(send, "head", split_axis=0, concat_axis=0, tiled=True)
    return got.transpose(1, 2, 0, 3).reshape(len(arrays), rows // parts, parts * chunk)


def per_device(
    q_soft, k_soft, v_soft, q_light, k_light, v_light, decay_log, norm_gain, doc_lengths
):
    parts = lax.axis_size("head")
    moved = to_heads([k_soft, v_soft, q_soft, q_light, k_light, v_light], parts)
    kv_soft = moved[:2]
    rest = moved[2:]
    heads_dev = decay_log.shape[0]
    row_count = kv_soft.shape[1]
    head_width = kv_soft.shape[2] // heads_dev
    light_out = lightning(
        rest[1], rest[2], rest[3], decay_log, norm_gain, row_count, heads_dev, head_width
    )
    soft_out = soft_attention(rest[0], kv_soft, doc_lengths, row_count, heads_dev, head_width)
    returned = to_tokens([soft_out, light_out], parts)
    return (returned[0], returned[1])


def solution(mesh):
    in_specs = (
        P(("ctx", "head"), None),
        P(("ctx", "head"), None),
        P(("ctx", "head"), None),
        P(("ctx", "head"), None),
        P(("ctx", "head"), None),
        P(("ctx", "head"), None),
        P("head", "ctx"),
        P("head"),
        P(),
    )
    out_specs = (P(("ctx", "head"), None), P(("ctx", "head"), None))
    return jax.shard_map(
        per_device, mesh=mesh, in_specs=in_specs, out_specs=out_specs, check_vma=False
    )
```

```python
from functools import partial

import jax
import jax.numpy as jnp
from jax import lax
from jax.experimental import pallas as pl
from jax.sharding import PartitionSpec as P

DOC_REACH = 8


def shifted(block, axis, distance):
    size = lax.axis_size(axis)
    route = [(i, (i + distance) % size) for i in range(size)]
    return lax.ppermute(block, axis, route)


def doc_index(positions, starts):
    return jnp.sum((positions[:, None] >= starts[None, :]).astype(jnp.int32), axis=1) - 1


def online_block_kernel(
    q_doc, k_doc, q_pos, k_pos, q_ref, kv_ref, m_in, l_in, acc_in, m_out, l_out, acc_out
):
    heads_dev = m_in.shape[0]
    rows = q_ref.shape[0]
    head_width = q_ref.shape[1] // heads_dev
    chunk = 128
    key_doc = k_doc[:1, :]
    key_pos = k_pos[:1, :]

    def body(i, carry):
        r = pl.ds(pl.multiple_of(i * chunk, chunk), chunk)
        allowed = (q_doc[r, :1] == key_doc) & (key_pos <= q_pos[r, :1])
        for h in range(heads_dev):
            cols = slice(h * head_width, (h + 1) * head_width)
            scores = lax.dot_general(
                q_ref[r, cols],
                kv_ref[0, :, cols],
                (((1,), (1,)), ((), ())),
                preferred_element_type=jnp.float32,
            )
            scores = jnp.where(allowed, scores * (1.0 / head_width**0.5), -1e30)
            run_max = m_in[h, r, :1]
            new_max = jnp.maximum(run_max, jnp.max(scores, axis=1, keepdims=True))
            correction = jnp.exp(run_max - new_max)
            probs = jnp.exp(scores - new_max)
            new_total = l_in[h, r, :1] * correction + jnp.sum(probs, axis=1, keepdims=True)
            product = jnp.dot(
                probs.astype(jnp.bfloat16), kv_ref[1, :, cols], preferred_element_type=jnp.float32
            )
            acc_out[r, cols] = acc_in[r, cols] * correction + product
            m_out[h, r, :] = jnp.broadcast_to(new_max, (chunk, m_out.shape[2]))
            l_out[h, r, :] = jnp.broadcast_to(new_total, (chunk, l_out.shape[2]))
        return carry

    lax.fori_loop(0, rows // chunk, body, 0)


def online_block(running, kv_pair, queries, query_doc, query_pos, key_doc, key_pos):
    run_max, run_total, run_acc = running
    rows, width = queries.shape
    heads_dev = run_max.shape[0]
    flops = 4 * rows * rows * width
    return pl.pallas_call(
        online_block_kernel,
        out_shape=(
            jax.ShapeDtypeStruct(run_max.shape, jnp.float32),
            jax.ShapeDtypeStruct(run_total.shape, jnp.float32),
            jax.ShapeDtypeStruct(run_acc.shape, jnp.float32),
        ),
        input_output_aliases={6: 0, 7: 1, 8: 2},
        cost_estimate=pl.CostEstimate(
            flops=flops, transcendentals=heads_dev * rows * rows, bytes_accessed=6 * rows * width * 4
        ),
    )(
        query_doc,
        key_doc,
        query_pos,
        key_pos,
        queries,
        kv_pair,
        run_max,
        run_total,
        run_acc,
    )


def soft_attention(q_rows, kv_pair, doc_lengths, row_count, heads_dev, head_width):
    size = lax.axis_size("ctx")
    own_index = lax.axis_index("ctx")
    reach = min(DOC_REACH, size - 1)
    forward_steps = (reach + 1) // 2
    starts = jnp.cumsum(doc_lengths) - doc_lengths
    query_pos = own_index * row_count + jnp.arange(row_count, dtype=jnp.int32)
    query_doc = doc_index(query_pos, starts)
    lanes = 128
    query_doc_wide = jnp.broadcast_to(query_doc[:, None], (row_count, lanes))
    query_pos_wide = jnp.broadcast_to(query_pos[:, None], (row_count, lanes))
    running = (
        jnp.full((heads_dev, row_count, lanes), -1e30, jnp.float32),
        jnp.zeros((heads_dev, row_count, lanes), jnp.float32),
        jnp.zeros((row_count, heads_dev * head_width), jnp.float32),
    )

    def absorb(running, block, source):
        key_pos = source * row_count + jnp.arange(row_count, dtype=jnp.int32)
        key_doc = doc_index(key_pos, starts)
        return online_block(
            running,
            block,
            q_rows,
            query_doc_wide,
            query_pos_wide,
            jnp.broadcast_to(key_doc[None, :], (8, row_count)),
            jnp.broadcast_to(key_pos[None, :], (8, row_count)),
        )

    def absorb_if_needed(running, block, offset):
        source = own_index - offset
        last_doc = doc_index(jnp.full((1,), source * row_count + row_count - 1, jnp.int32), starts)[
            0
        ]
        needed = (source >= 0) & (last_doc == query_doc[0])
        return lax.cond(
            needed, lambda r: absorb(r, block, source), lambda r: r, running
        )

    fwd_offsets = list(range(1, forward_steps + 1))
    bwd_offsets = list(range(reach, forward_steps, -1))
    running = absorb(running, kv_pair, own_index)
    ahead = shifted(kv_pair, "ctx", 1)
    behind = shifted(kv_pair, "ctx", reach) if bwd_offsets else None
    for i in range(max(len(fwd_offsets), len(bwd_offsets))):
        if i == 0:
            ahead, running = lax.optimization_barrier((ahead, running))
        ahead_next = shifted(ahead, "ctx", 1) if i + 1 < len(fwd_offsets) else None
        behind_next = shifted(behind, "ctx", -1) if i + 1 < len(bwd_offsets) else None
        if i < len(fwd_offsets):
            running = absorb_if_needed(running, ahead, fwd_offsets[i])
        if i < len(bwd_offsets):
            running = absorb_if_needed(running, behind, bwd_offsets[i])
        ahead_next, behind_next, running = lax.optimization_barrier(
            (ahead_next, behind_next, running)
        )
        ahead, behind = ahead_next, behind_next
    run_max, run_total, run_acc = running
    totals = run_total[:, :, 0].T
    mixed = run_acc.reshape(row_count, heads_dev, head_width) / totals[:, :, None]
    return mixed.astype(jnp.bfloat16).reshape(row_count, heads_dev * head_width)


def lightning(q_rows, k_rows, v_rows, decay_log, norm_gain, row_count, heads_dev, head_width):
    size = lax.axis_size("ctx")
    own_index = lax.axis_index("ctx")
    cumul = jnp.cumsum(decay_log, axis=1)
    block_end = cumul[:, -1:]
    queries = q_rows.reshape(row_count, heads_dev, head_width)
    keys_here = k_rows.reshape(row_count, heads_dev, head_width)
    vals_here = v_rows.reshape(row_count, heads_dev, head_width)
    weighted = (keys_here * jnp.exp(block_end - cumul).T[:, :, None]).astype(jnp.bfloat16)
    update = jnp.einsum("thd,the->hde", weighted, vals_here, preferred_element_type=jnp.float32)
    end_hi = block_end.astype(jnp.bfloat16)
    end_lo = (block_end - end_hi.astype(jnp.float32)).astype(jnp.bfloat16)
    extra = jnp.zeros((heads_dev, 16, head_width), jnp.bfloat16)
    extra = extra.at[:, 0, :].set(jnp.broadcast_to(end_hi, (heads_dev, head_width)))
    extra = extra.at[:, 1, :].set(jnp.broadcast_to(end_lo, (heads_dev, head_width)))
    packed = jnp.concatenate([update.astype(jnp.bfloat16), extra], axis=1)
    gathered = lax.all_gather(packed, "ctx")
    ends = gathered[:, :, head_width, 0].astype(jnp.float32) + gathered[
        :, :, head_width + 1, 0
    ].astype(jnp.float32)
    blocks = jnp.arange(size, dtype=jnp.int32)
    between = (blocks[:, None] < blocks[None, :]) & (blocks[None, :] < own_index)
    exponent = jnp.einsum(
        "cb,bh->ch", between.astype(jnp.float32), ends, precision=lax.Precision.HIGHEST
    )
    weight = jnp.where((blocks < own_index)[:, None], jnp.exp(exponent), 0.0)
    entering = jnp.einsum(
        "ch,chde->hde",
        weight,
        gathered[:, :, :head_width, :].astype(jnp.float32),
        precision=lax.Precision.HIGHEST,
    )
    state_low = entering.astype(jnp.bfloat16)
    token_ids = jnp.arange(row_count, dtype=jnp.int32)
    causal = token_ids[None, :] <= token_ids[:, None]
    log_gap = jnp.where(causal[None], cumul[:, :, None] - cumul[:, None, :], -jnp.inf)
    raw_scores = jnp.einsum("thd,shd->hts", queries, keys_here, preferred_element_type=jnp.float32)
    gated = (raw_scores * jnp.exp(log_gap)).astype(jnp.bfloat16)
    inner = jnp.einsum("hts,shd->thd", gated, vals_here, preferred_element_type=jnp.float32)
    outer = (
        jnp.einsum("thd,hde->the", queries, state_low, preferred_element_type=jnp.float32)
        * jnp.exp(cumul).T[:, :, None]
    )
    raw_out = inner + outer
    mean_sq = jnp.mean(raw_out * raw_out, axis=2, keepdims=True)
    normed = raw_out * lax.rsqrt(mean_sq + 1e-06) * norm_gain.reshape(heads_dev, head_width)[None]
    return normed.astype(jnp.bfloat16).reshape(row_count, heads_dev * head_width)


def to_heads(arrays, parts):
    rows, width = arrays[0].shape
    chunk = width // parts
    send = jnp.stack([a.reshape(rows, parts, chunk) for a in arrays], axis=1)
    send = send.transpose(2, 1, 0, 3)
    got = lax.all_to_all(send, "head", split_axis=0, concat_axis=0, tiled=True)
    return got.transpose(1, 0, 2, 3).reshape(len(arrays), parts * rows, chunk)


def to_tokens(arrays, parts):
    rows, chunk = arrays[0].shape
    send = jnp.stack([a.reshape(parts, rows // parts, chunk) for a in arrays], axis=1)
    got = lax.all_to_all(send, "head", split_axis=0, concat_axis=0, tiled=True)
    return got.transpose(1, 2, 0, 3).reshape(len(arrays), rows // parts, parts * chunk)


def per_device(
    q_soft, k_soft, v_soft, q_light, k_light, v_light, decay_log, norm_gain, doc_lengths
):
    parts = lax.axis_size("head")
    moved = to_heads([k_soft, v_soft, q_soft, q_light, k_light, v_light], parts)
    kv_soft = moved[:2]
    rest = moved[2:]
    heads_dev = decay_log.shape[0]
    row_count = kv_soft.shape[1]
    head_width = kv_soft.shape[2] // heads_dev
    light_out = lightning(
        rest[1], rest[2], rest[3], decay_log, norm_gain, row_count, heads_dev, head_width
    )
    soft_out = soft_attention(rest[0], kv_soft, doc_lengths, row_count, heads_dev, head_width)
    light_back = to_tokens([light_out], parts)[0]
    soft_back = to_tokens([soft_out], parts)[0]
    return (soft_back, light_back)


def solution(mesh):
    in_specs = (
        P(("ctx", "head"), None),
        P(("ctx", "head"), None),
        P(("ctx", "head"), None),
        P(("ctx", "head"), None),
        P(("ctx", "head"), None),
        P(("ctx", "head"), None),
        P("head", "ctx"),
        P("head"),
        P(),
    )
    out_specs = (P(("ctx", "head"), None), P(("ctx", "head"), None))
    return jax.shard_map(
        per_device, mesh=mesh, in_specs=in_specs, out_specs=out_specs, check_vma=False
    )
```

```python
from functools import partial

import jax
import jax.numpy as jnp
from jax import lax
from jax.experimental import pallas as pl
from jax.sharding import PartitionSpec as P

DOC_REACH = 8


def shifted(block, axis, distance):
    size = lax.axis_size(axis)
    route = [(i, (i + distance) % size) for i in range(size)]
    return lax.ppermute(block, axis, route)


def doc_index(positions, starts):
    return jnp.sum((positions[:, None] >= starts[None, :]).astype(jnp.int32), axis=1) - 1


def online_block_kernel(
    q_doc, k_doc, q_pos, k_pos, q_ref, kv_ref, m_in, l_in, acc_in, m_out, l_out, acc_out
):
    heads_dev = m_in.shape[0]
    rows = q_ref.shape[0]
    head_width = q_ref.shape[1] // heads_dev
    chunk = 128
    key_doc = k_doc[:1, :]
    key_pos = k_pos[:1, :]

    def body(i, carry):
        r = pl.ds(pl.multiple_of(i * chunk, chunk), chunk)
        allowed = (q_doc[r, :1] == key_doc) & (key_pos <= q_pos[r, :1])
        for h in range(heads_dev):
            cols = slice(h * head_width, (h + 1) * head_width)
            scores = lax.dot_general(
                q_ref[r, cols],
                kv_ref[0, :, cols],
                (((1,), (1,)), ((), ())),
                preferred_element_type=jnp.float32,
            )
            scores = jnp.where(allowed, scores * (1.0 / head_width**0.5), -1e30)
            run_max = m_in[h, r, :1]
            new_max = jnp.maximum(run_max, jnp.max(scores, axis=1, keepdims=True))
            correction = jnp.exp(run_max - new_max)
            probs = jnp.exp(scores - new_max)
            new_total = l_in[h, r, :1] * correction + jnp.sum(probs, axis=1, keepdims=True)
            product = jnp.dot(
                probs.astype(jnp.bfloat16), kv_ref[1, :, cols], preferred_element_type=jnp.float32
            )
            acc_out[r, cols] = acc_in[r, cols] * correction + product
            m_out[h, r, :] = jnp.broadcast_to(new_max, (chunk, m_out.shape[2]))
            l_out[h, r, :] = jnp.broadcast_to(new_total, (chunk, l_out.shape[2]))
        return carry

    lax.fori_loop(0, rows // chunk, body, 0)


def online_block(running, kv_pair, queries, query_doc, query_pos, key_doc, key_pos):
    run_max, run_total, run_acc = running
    rows, width = queries.shape
    heads_dev = run_max.shape[0]
    flops = 4 * rows * rows * width
    return pl.pallas_call(
        online_block_kernel,
        out_shape=(
            jax.ShapeDtypeStruct(run_max.shape, jnp.float32),
            jax.ShapeDtypeStruct(run_total.shape, jnp.float32),
            jax.ShapeDtypeStruct(run_acc.shape, jnp.float32),
        ),
        input_output_aliases={6: 0, 7: 1, 8: 2},
        cost_estimate=pl.CostEstimate(
            flops=flops, transcendentals=heads_dev * rows * rows, bytes_accessed=6 * rows * width * 4
        ),
    )(
        query_doc,
        key_doc,
        query_pos,
        key_pos,
        queries,
        kv_pair,
        run_max,
        run_total,
        run_acc,
    )


def soft_attention(q_rows, kv_pair, doc_lengths, row_count, heads_dev, head_width):
    size = lax.axis_size("ctx")
    own_index = lax.axis_index("ctx")
    reach = min(DOC_REACH, size - 1)
    forward_steps = (reach + 1) // 2
    starts = jnp.cumsum(doc_lengths) - doc_lengths
    query_pos = own_index * row_count + jnp.arange(row_count, dtype=jnp.int32)
    query_doc = doc_index(query_pos, starts)
    lanes = 128
    query_doc_wide = jnp.broadcast_to(query_doc[:, None], (row_count, lanes))
    query_pos_wide = jnp.broadcast_to(query_pos[:, None], (row_count, lanes))
    running = (
        jnp.full((heads_dev, row_count, lanes), -1e30, jnp.float32),
        jnp.zeros((heads_dev, row_count, lanes), jnp.float32),
        jnp.zeros((row_count, heads_dev * head_width), jnp.float32),
    )

    def absorb(running, block, source):
        key_pos = source * row_count + jnp.arange(row_count, dtype=jnp.int32)
        key_doc = doc_index(key_pos, starts)
        return online_block(
            running,
            block,
            q_rows,
            query_doc_wide,
            query_pos_wide,
            jnp.broadcast_to(key_doc[None, :], (8, row_count)),
            jnp.broadcast_to(key_pos[None, :], (8, row_count)),
        )

    def absorb_if_needed(running, block, offset):
        source = own_index - offset
        last_doc = doc_index(jnp.full((1,), source * row_count + row_count - 1, jnp.int32), starts)[
            0
        ]
        needed = (source >= 0) & (last_doc == query_doc[0])
        return lax.cond(
            needed, lambda r: absorb(r, block, source), lambda r: r, running
        )

    fwd_offsets = list(range(1, forward_steps + 1))
    bwd_offsets = list(range(reach, forward_steps, -1))
    running = absorb(running, kv_pair, own_index)
    ahead = shifted(kv_pair, "ctx", 1)
    behind = shifted(kv_pair, "ctx", reach) if bwd_offsets else None
    for i in range(max(len(fwd_offsets), len(bwd_offsets))):
        if i == 0:
            ahead, running = lax.optimization_barrier((ahead, running))
        ahead_next = shifted(ahead, "ctx", 1) if i + 1 < len(fwd_offsets) else None
        behind_next = shifted(behind, "ctx", -1) if i + 1 < len(bwd_offsets) else None
        if i < len(fwd_offsets):
            running = absorb_if_needed(running, ahead, fwd_offsets[i])
        if i < len(bwd_offsets):
            running = absorb_if_needed(running, behind, bwd_offsets[i])
        ahead_next, behind_next, running = lax.optimization_barrier(
            (ahead_next, behind_next, running)
        )
        ahead, behind = ahead_next, behind_next
    run_max, run_total, run_acc = running
    totals = run_total[:, :, 0].T
    mixed = run_acc.reshape(row_count, heads_dev, head_width) / totals[:, :, None]
    return mixed.astype(jnp.bfloat16).reshape(row_count, heads_dev * head_width)


def lightning(q_rows, k_rows, v_rows, decay_log, norm_gain, row_count, heads_dev, head_width):
    size = lax.axis_size("ctx")
    own_index = lax.axis_index("ctx")
    cumul = jnp.cumsum(decay_log, axis=1)
    block_end = cumul[:, -1:]
    queries = q_rows.reshape(row_count, heads_dev, head_width)
    keys_here = k_rows.reshape(row_count, heads_dev, head_width)
    vals_here = v_rows.reshape(row_count, heads_dev, head_width)
    weighted = (keys_here * jnp.exp(block_end - cumul).T[:, :, None]).astype(jnp.bfloat16)
    update = jnp.einsum("thd,the->hde", weighted, vals_here, preferred_element_type=jnp.float32)
    carried = jnp.concatenate(
        [update, jnp.broadcast_to(block_end[:, :, None], (heads_dev, 8, head_width))], axis=1
    )
    shift = 1
    while shift < size:
        route = [(i, i + shift) for i in range(size - shift)]
        earlier = lax.ppermute(carried, "ctx", route)
        own_log = carried[:, head_width, 0]
        state = jnp.exp(own_log)[:, None, None] * earlier[:, :head_width] + carried[:, :head_width]
        logs = earlier[:, head_width:] + carried[:, head_width:]
        carried = jnp.concatenate([state, logs], axis=1)
        shift *= 2
    entering = lax.ppermute(carried, "ctx", [(i, i + 1) for i in range(size - 1)])[:, :head_width]
    state_low = entering.astype(jnp.bfloat16)
    token_ids = jnp.arange(row_count, dtype=jnp.int32)
    causal = token_ids[None, :] <= token_ids[:, None]
    log_gap = jnp.where(causal[None], cumul[:, :, None] - cumul[:, None, :], -jnp.inf)
    raw_scores = jnp.einsum("thd,shd->hts", queries, keys_here, preferred_element_type=jnp.float32)
    gated = (raw_scores * jnp.exp(log_gap)).astype(jnp.bfloat16)
    inner = jnp.einsum("hts,shd->thd", gated, vals_here, preferred_element_type=jnp.float32)
    outer = (
        jnp.einsum("thd,hde->the", queries, state_low, preferred_element_type=jnp.float32)
        * jnp.exp(cumul).T[:, :, None]
    )
    raw_out = inner + outer
    mean_sq = jnp.mean(raw_out * raw_out, axis=2, keepdims=True)
    normed = raw_out * lax.rsqrt(mean_sq + 1e-06) * norm_gain.reshape(heads_dev, head_width)[None]
    return normed.astype(jnp.bfloat16).reshape(row_count, heads_dev * head_width)


def to_heads(arrays, parts):
    rows, width = arrays[0].shape
    chunk = width // parts
    send = jnp.stack([a.reshape(rows, parts, chunk) for a in arrays], axis=1)
    send = send.transpose(2, 1, 0, 3)
    got = lax.all_to_all(send, "head", split_axis=0, concat_axis=0, tiled=True)
    return got.transpose(1, 0, 2, 3).reshape(len(arrays), parts * rows, chunk)


def to_tokens(arrays, parts):
    rows, chunk = arrays[0].shape
    send = jnp.stack([a.reshape(parts, rows // parts, chunk) for a in arrays], axis=1)
    got = lax.all_to_all(send, "head", split_axis=0, concat_axis=0, tiled=True)
    return got.transpose(1, 2, 0, 3).reshape(len(arrays), rows // parts, parts * chunk)


def per_device(
    q_soft, k_soft, v_soft, q_light, k_light, v_light, decay_log, norm_gain, doc_lengths
):
    parts = lax.axis_size("head")
    moved = to_heads([k_soft, v_soft, q_soft, q_light, k_light, v_light], parts)
    kv_soft = moved[:2]
    rest = moved[2:]
    heads_dev = decay_log.shape[0]
    row_count = kv_soft.shape[1]
    head_width = kv_soft.shape[2] // heads_dev
    light_out = lightning(
        rest[1], rest[2], rest[3], decay_log, norm_gain, row_count, heads_dev, head_width
    )
    soft_out = soft_attention(rest[0], kv_soft, doc_lengths, row_count, heads_dev, head_width)
    returned = to_tokens([soft_out, light_out], parts)
    return (returned[0], returned[1])


def solution(mesh):
    in_specs = (
        P(("ctx", "head"), None),
        P(("ctx", "head"), None),
        P(("ctx", "head"), None),
        P(("ctx", "head"), None),
        P(("ctx", "head"), None),
        P(("ctx", "head"), None),
        P("head", "ctx"),
        P("head"),
        P(),
    )
    out_specs = (P(("ctx", "head"), None), P(("ctx", "head"), None))
    return jax.shard_map(
        per_device, mesh=mesh, in_specs=in_specs, out_specs=out_specs, check_vma=False
    )
```

```python
from functools import partial

import jax
import jax.numpy as jnp
from jax import lax
from jax.experimental import pallas as pl
from jax.sharding import PartitionSpec as P

DOC_REACH = 8


def shifted(block, axis, distance):
    size = lax.axis_size(axis)
    route = [(i, (i + distance) % size) for i in range(size)]
    return lax.ppermute(block, axis, route)


def doc_index(positions, starts):
    return jnp.sum((positions[:, None] >= starts[None, :]).astype(jnp.int32), axis=1) - 1


def online_block_kernel(
    q_doc, k_doc, q_pos, k_pos, q_ref, kv_ref, m_in, l_in, acc_in, m_out, l_out, acc_out
):
    heads_dev = m_in.shape[0]
    rows = q_ref.shape[0]
    head_width = q_ref.shape[1] // heads_dev
    chunk = 128
    key_doc = k_doc[:1, :]
    key_pos = k_pos[:1, :]

    def body(i, carry):
        r = pl.ds(pl.multiple_of(i * chunk, chunk), chunk)
        allowed = (q_doc[r, :1] == key_doc) & (key_pos <= q_pos[r, :1])
        for h in range(heads_dev):
            cols = slice(h * head_width, (h + 1) * head_width)
            scores = lax.dot_general(
                q_ref[r, cols],
                kv_ref[0, :, cols],
                (((1,), (1,)), ((), ())),
                preferred_element_type=jnp.float32,
            )
            scores = jnp.where(allowed, scores * (1.0 / head_width**0.5), -1e30)
            run_max = m_in[h, r, :1]
            new_max = jnp.maximum(run_max, jnp.max(scores, axis=1, keepdims=True))
            correction = jnp.exp(run_max - new_max)
            probs = jnp.exp(scores - new_max)
            new_total = l_in[h, r, :1] * correction + jnp.sum(probs, axis=1, keepdims=True)
            product = jnp.dot(
                probs.astype(jnp.bfloat16), kv_ref[1, :, cols], preferred_element_type=jnp.float32
            )
            acc_out[r, cols] = acc_in[r, cols] * correction + product
            m_out[h, r, :] = jnp.broadcast_to(new_max, (chunk, m_out.shape[2]))
            l_out[h, r, :] = jnp.broadcast_to(new_total, (chunk, l_out.shape[2]))
        return carry

    lax.fori_loop(0, rows // chunk, body, 0)


def online_block(running, kv_pair, queries, query_doc, query_pos, key_doc, key_pos):
    run_max, run_total, run_acc = running
    rows, width = queries.shape
    heads_dev = run_max.shape[0]
    flops = 4 * rows * rows * width
    return pl.pallas_call(
        online_block_kernel,
        out_shape=(
            jax.ShapeDtypeStruct(run_max.shape, jnp.float32),
            jax.ShapeDtypeStruct(run_total.shape, jnp.float32),
            jax.ShapeDtypeStruct(run_acc.shape, jnp.float32),
        ),
        input_output_aliases={6: 0, 7: 1, 8: 2},
        cost_estimate=pl.CostEstimate(
            flops=flops, transcendentals=heads_dev * rows * rows, bytes_accessed=6 * rows * width * 4
        ),
    )(
        query_doc,
        key_doc,
        query_pos,
        key_pos,
        queries,
        kv_pair,
        run_max,
        run_total,
        run_acc,
    )


def soft_attention(q_rows, kv_pair, doc_lengths, row_count, heads_dev, head_width):
    size = lax.axis_size("ctx")
    own_index = lax.axis_index("ctx")
    reach = min(DOC_REACH, size - 1)
    forward_steps = (reach + 1) // 2
    starts = jnp.cumsum(doc_lengths) - doc_lengths
    query_pos = own_index * row_count + jnp.arange(row_count, dtype=jnp.int32)
    query_doc = doc_index(query_pos, starts)
    lanes = 128
    query_doc_wide = jnp.broadcast_to(query_doc[:, None], (row_count, lanes))
    query_pos_wide = jnp.broadcast_to(query_pos[:, None], (row_count, lanes))
    running = (
        jnp.full((heads_dev, row_count, lanes), -1e30, jnp.float32),
        jnp.zeros((heads_dev, row_count, lanes), jnp.float32),
        jnp.zeros((row_count, heads_dev * head_width), jnp.float32),
    )

    def absorb(running, block, source):
        key_pos = source * row_count + jnp.arange(row_count, dtype=jnp.int32)
        key_doc = doc_index(key_pos, starts)
        return online_block(
            running,
            block,
            q_rows,
            query_doc_wide,
            query_pos_wide,
            jnp.broadcast_to(key_doc[None, :], (8, row_count)),
            jnp.broadcast_to(key_pos[None, :], (8, row_count)),
        )

    def absorb_if_needed(running, block, offset):
        source = own_index - offset
        last_doc = doc_index(jnp.full((1,), source * row_count + row_count - 1, jnp.int32), starts)[
            0
        ]
        needed = (source >= 0) & (last_doc == query_doc[0])
        return lax.cond(
            needed, lambda r: absorb(r, block, source), lambda r: r, running
        )

    fwd_offsets = list(range(1, forward_steps + 1))
    bwd_offsets = list(range(reach, forward_steps, -1))
    running = absorb(running, kv_pair, own_index)
    ahead = shifted(kv_pair, "ctx", 1)
    behind = shifted(kv_pair, "ctx", reach) if bwd_offsets else None
    for i in range(max(len(fwd_offsets), len(bwd_offsets))):
        if i == 0:
            ahead, running = lax.optimization_barrier((ahead, running))
        ahead_next = shifted(ahead, "ctx", 1) if i + 1 < len(fwd_offsets) else None
        behind_next = shifted(behind, "ctx", -1) if i + 1 < len(bwd_offsets) else None
        if i < len(fwd_offsets):
            running = absorb_if_needed(running, ahead, fwd_offsets[i])
        if i < len(bwd_offsets):
            running = absorb_if_needed(running, behind, bwd_offsets[i])
        ahead_next, behind_next, running = lax.optimization_barrier(
            (ahead_next, behind_next, running)
        )
        ahead, behind = ahead_next, behind_next
    run_max, run_total, run_acc = running
    totals = run_total[:, :, 0].T
    mixed = run_acc.reshape(row_count, heads_dev, head_width) / totals[:, :, None]
    return mixed.astype(jnp.bfloat16).reshape(row_count, heads_dev * head_width)


def lightning(q_rows, k_rows, v_rows, decay_log, norm_gain, row_count, heads_dev, head_width):
    size = lax.axis_size("ctx")
    own_index = lax.axis_index("ctx")
    cumul = jnp.cumsum(decay_log, axis=1)
    block_end = cumul[:, -1:]
    queries = q_rows.reshape(row_count, heads_dev, head_width)
    keys_here = k_rows.reshape(row_count, heads_dev, head_width)
    vals_here = v_rows.reshape(row_count, heads_dev, head_width)
    weighted = (keys_here * jnp.exp(block_end - cumul).T[:, :, None]).astype(jnp.bfloat16)
    update = jnp.einsum("thd,the->hde", weighted, vals_here, preferred_element_type=jnp.float32)
    end_hi = block_end.astype(jnp.bfloat16)
    end_lo = (block_end - end_hi.astype(jnp.float32)).astype(jnp.bfloat16)
    extra = jnp.zeros((heads_dev, 16, head_width), jnp.bfloat16)
    extra = extra.at[:, 0, :].set(jnp.broadcast_to(end_hi, (heads_dev, head_width)))
    extra = extra.at[:, 1, :].set(jnp.broadcast_to(end_lo, (heads_dev, head_width)))
    packed = jnp.concatenate([update.astype(jnp.bfloat16), extra], axis=1)
    gathered = lax.all_gather(packed, "ctx")
    ends = gathered[:, :, head_width, 0].astype(jnp.float32) + gathered[
        :, :, head_width + 1, 0
    ].astype(jnp.float32)
    blocks = jnp.arange(size, dtype=jnp.int32)
    between = (blocks[:, None] < blocks[None, :]) & (blocks[None, :] < own_index)
    exponent = jnp.einsum(
        "cb,bh->ch", between.astype(jnp.float32), ends, precision=lax.Precision.HIGHEST
    )
    weight = jnp.where((blocks < own_index)[:, None], jnp.exp(exponent), 0.0)
    entering = jnp.einsum(
        "ch,chde->hde",
        weight,
        gathered[:, :, :head_width, :].astype(jnp.float32),
        precision=lax.Precision.HIGHEST,
    )
    state_low = entering.astype(jnp.bfloat16)
    token_ids = jnp.arange(row_count, dtype=jnp.int32)
    causal = token_ids[None, :] <= token_ids[:, None]
    log_gap = jnp.where(causal[None], cumul[:, :, None] - cumul[:, None, :], -jnp.inf)
    raw_scores = jnp.einsum("thd,shd->hts", queries, keys_here, preferred_element_type=jnp.float32)
    gated = (raw_scores * jnp.exp(log_gap)).astype(jnp.bfloat16)
    inner = jnp.einsum("hts,shd->thd", gated, vals_here, preferred_element_type=jnp.float32)
    outer = (
        jnp.einsum("thd,hde->the", queries, state_low, preferred_element_type=jnp.float32)
        * jnp.exp(cumul).T[:, :, None]
    )
    raw_out = inner + outer
    mean_sq = jnp.mean(raw_out * raw_out, axis=2, keepdims=True)
    normed = raw_out * lax.rsqrt(mean_sq + 1e-06) * norm_gain.reshape(heads_dev, head_width)[None]
    return normed.astype(jnp.bfloat16).reshape(row_count, heads_dev * head_width)


def to_heads(arrays, parts):
    rows, width = arrays[0].shape
    chunk = width // parts
    send = jnp.stack([a.reshape(rows, parts, chunk) for a in arrays], axis=1)
    send = send.transpose(2, 1, 0, 3)
    got = lax.all_to_all(send, "head", split_axis=0, concat_axis=0, tiled=True)
    return got.transpose(1, 0, 2, 3).reshape(len(arrays), parts * rows, chunk)


def to_tokens(arrays, parts):
    rows, chunk = arrays[0].shape
    send = jnp.stack([a.reshape(parts, rows // parts, chunk) for a in arrays], axis=1)
    got = lax.all_to_all(send, "head", split_axis=0, concat_axis=0, tiled=True)
    return got.transpose(1, 2, 0, 3).reshape(len(arrays), rows // parts, parts * chunk)


def per_device(
    q_soft, k_soft, v_soft, q_light, k_light, v_light, decay_log, norm_gain, doc_lengths
):
    parts = lax.axis_size("head")
    moved = to_heads([k_soft, v_soft, q_soft, q_light, k_light, v_light], parts)
    kv_soft = moved[:2]
    rest = moved[2:]
    heads_dev = decay_log.shape[0]
    row_count = kv_soft.shape[1]
    head_width = kv_soft.shape[2] // heads_dev
    light_out = lightning(
        rest[1], rest[2], rest[3], decay_log, norm_gain, row_count, heads_dev, head_width
    )
    soft_out = soft_attention(rest[0], kv_soft, doc_lengths, row_count, heads_dev, head_width)
    returned = to_tokens([soft_out, light_out], parts)
    return (returned[0], returned[1])


def solution(mesh):
    in_specs = (
        P(("ctx", "head"), None),
        P(("ctx", "head"), None),
        P(("ctx", "head"), None),
        P(("ctx", "head"), None),
        P(("ctx", "head"), None),
        P(("ctx", "head"), None),
        P("head", "ctx"),
        P("head"),
        P(),
    )
    out_specs = (P(("ctx", "head"), None), P(("ctx", "head"), None))
    return jax.shard_map(
        per_device, mesh=mesh, in_specs=in_specs, out_specs=out_specs, check_vma=False
    )
```

```python
from functools import partial

import jax
import jax.numpy as jnp
from jax import lax
from jax.experimental import pallas as pl
from jax.sharding import PartitionSpec as P

DOC_REACH = 8


def shifted(block, axis, distance):
    size = lax.axis_size(axis)
    route = [(i, (i + distance) % size) for i in range(size)]
    return lax.ppermute(block, axis, route)


def doc_index(positions, starts):
    return jnp.sum((positions[:, None] >= starts[None, :]).astype(jnp.int32), axis=1) - 1


def online_block_kernel(
    q_doc, k_doc, q_pos, k_pos, q_ref, kv_ref, m_in, l_in, acc_in, m_out, l_out, acc_out
):
    heads_dev = m_in.shape[0]
    rows = q_ref.shape[0]
    head_width = q_ref.shape[1] // heads_dev
    chunk = 128
    key_doc = k_doc[:1, :]
    key_pos = k_pos[:1, :]

    def body(i, carry):
        r = pl.ds(pl.multiple_of(i * chunk, chunk), chunk)
        allowed = (q_doc[r, :1] == key_doc) & (key_pos <= q_pos[r, :1])
        for h in range(heads_dev):
            cols = slice(h * head_width, (h + 1) * head_width)
            scores = lax.dot_general(
                q_ref[r, cols],
                kv_ref[0, :, cols],
                (((1,), (1,)), ((), ())),
                preferred_element_type=jnp.float32,
            )
            scores = jnp.where(allowed, scores * (1.0 / head_width**0.5), -1e30)
            run_max = m_in[h, r, :1]
            new_max = jnp.maximum(run_max, jnp.max(scores, axis=1, keepdims=True))
            correction = jnp.exp(run_max - new_max)
            probs = jnp.exp(scores - new_max)
            new_total = l_in[h, r, :1] * correction + jnp.sum(probs, axis=1, keepdims=True)
            product = jnp.dot(
                probs.astype(jnp.bfloat16), kv_ref[1, :, cols], preferred_element_type=jnp.float32
            )
            acc_out[r, cols] = acc_in[r, cols] * correction + product
            m_out[h, r, :] = jnp.broadcast_to(new_max, (chunk, m_out.shape[2]))
            l_out[h, r, :] = jnp.broadcast_to(new_total, (chunk, l_out.shape[2]))
        return carry

    lax.fori_loop(0, rows // chunk, body, 0)


def online_block(running, kv_pair, queries, query_doc, query_pos, key_doc, key_pos):
    run_max, run_total, run_acc = running
    rows, width = queries.shape
    heads_dev = run_max.shape[0]
    flops = 4 * rows * rows * width
    return pl.pallas_call(
        online_block_kernel,
        out_shape=(
            jax.ShapeDtypeStruct(run_max.shape, jnp.float32),
            jax.ShapeDtypeStruct(run_total.shape, jnp.float32),
            jax.ShapeDtypeStruct(run_acc.shape, jnp.float32),
        ),
        input_output_aliases={6: 0, 7: 1, 8: 2},
        cost_estimate=pl.CostEstimate(
            flops=flops, transcendentals=heads_dev * rows * rows, bytes_accessed=6 * rows * width * 4
        ),
    )(
        query_doc,
        key_doc,
        query_pos,
        key_pos,
        queries,
        kv_pair,
        run_max,
        run_total,
        run_acc,
    )


def soft_attention(q_rows, kv_pair, doc_lengths, row_count, heads_dev, head_width):
    size = lax.axis_size("ctx")
    own_index = lax.axis_index("ctx")
    reach = min(DOC_REACH, size - 1)
    forward_steps = (reach + 1) // 2
    starts = jnp.cumsum(doc_lengths) - doc_lengths
    query_pos = own_index * row_count + jnp.arange(row_count, dtype=jnp.int32)
    query_doc = doc_index(query_pos, starts)
    lanes = 128
    query_doc_wide = jnp.broadcast_to(query_doc[:, None], (row_count, lanes))
    query_pos_wide = jnp.broadcast_to(query_pos[:, None], (row_count, lanes))
    running = (
        jnp.full((heads_dev, row_count, lanes), -1e30, jnp.float32),
        jnp.zeros((heads_dev, row_count, lanes), jnp.float32),
        jnp.zeros((row_count, heads_dev * head_width), jnp.float32),
    )

    fwd_offsets = list(range(1, forward_steps + 1))
    bwd_offsets = list(range(reach, forward_steps, -1))
    offsets = [0] + fwd_offsets + bwd_offsets
    sources = own_index - jnp.array(offsets, jnp.int32)
    key_pos_all = sources[:, None] * row_count + jnp.arange(row_count, dtype=jnp.int32)[None, :]
    key_doc_all = doc_index(key_pos_all.reshape(-1), starts).reshape(len(offsets), row_count)
    needed_all = (sources >= 0) & (key_doc_all[:, -1] == query_doc[0])
    needed_all = needed_all | (sources == own_index)
    key_doc_all = jnp.where(needed_all[:, None], key_doc_all, -1)
    key_doc_tab = jnp.broadcast_to(key_doc_all[:, None, :], (len(offsets), 8, row_count))
    key_pos_tab = jnp.broadcast_to(key_pos_all[:, None, :], (len(offsets), 8, row_count))
    slot = {offset: j for j, offset in enumerate(offsets)}

    def absorb(running, block, offset):
        j = slot[offset]
        return online_block(
            running, block, q_rows, query_doc_wide, query_pos_wide, key_doc_tab[j], key_pos_tab[j]
        )

    running = absorb(running, kv_pair, 0)
    ahead = shifted(kv_pair, "ctx", 1)
    behind = shifted(kv_pair, "ctx", reach) if bwd_offsets else None
    for i in range(max(len(fwd_offsets), len(bwd_offsets))):
        if i == 0:
            ahead, running = lax.optimization_barrier((ahead, running))
        ahead_next = shifted(ahead, "ctx", 1) if i + 1 < len(fwd_offsets) else None
        behind_next = shifted(behind, "ctx", -1) if i + 1 < len(bwd_offsets) else None
        if i < len(fwd_offsets):
            running = absorb(running, ahead, fwd_offsets[i])
        if i < len(bwd_offsets):
            running = absorb(running, behind, bwd_offsets[i])
        ahead_next, behind_next, running = lax.optimization_barrier(
            (ahead_next, behind_next, running)
        )
        ahead, behind = ahead_next, behind_next
    run_max, run_total, run_acc = running
    totals = run_total[:, :, 0].T
    mixed = run_acc.reshape(row_count, heads_dev, head_width) / totals[:, :, None]
    return mixed.astype(jnp.bfloat16).reshape(row_count, heads_dev * head_width)


def lightning(q_rows, k_rows, v_rows, decay_log, norm_gain, row_count, heads_dev, head_width):
    size = lax.axis_size("ctx")
    own_index = lax.axis_index("ctx")
    cumul = jnp.cumsum(decay_log, axis=1)
    block_end = cumul[:, -1:]
    queries = q_rows.reshape(row_count, heads_dev, head_width)
    keys_here = k_rows.reshape(row_count, heads_dev, head_width)
    vals_here = v_rows.reshape(row_count, heads_dev, head_width)
    weighted = (keys_here * jnp.exp(block_end - cumul).T[:, :, None]).astype(jnp.bfloat16)
    update = jnp.einsum("thd,the->hde", weighted, vals_here, preferred_element_type=jnp.float32)
    end_hi = block_end.astype(jnp.bfloat16)
    end_lo = (block_end - end_hi.astype(jnp.float32)).astype(jnp.bfloat16)
    extra = jnp.zeros((heads_dev, 16, head_width), jnp.bfloat16)
    extra = extra.at[:, 0, :].set(jnp.broadcast_to(end_hi, (heads_dev, head_width)))
    extra = extra.at[:, 1, :].set(jnp.broadcast_to(end_lo, (heads_dev, head_width)))
    packed = jnp.concatenate([update.astype(jnp.bfloat16), extra], axis=1)
    gathered = lax.all_gather(packed, "ctx")
    ends = gathered[:, :, head_width, 0].astype(jnp.float32) + gathered[
        :, :, head_width + 1, 0
    ].astype(jnp.float32)
    blocks = jnp.arange(size, dtype=jnp.int32)
    between = (blocks[:, None] < blocks[None, :]) & (blocks[None, :] < own_index)
    exponent = jnp.einsum(
        "cb,bh->ch", between.astype(jnp.float32), ends, precision=lax.Precision.HIGHEST
    )
    weight = jnp.where((blocks < own_index)[:, None], jnp.exp(exponent), 0.0)
    entering = jnp.einsum(
        "ch,chde->hde",
        weight,
        gathered[:, :, :head_width, :].astype(jnp.float32),
        precision=lax.Precision.HIGHEST,
    )
    state_low = entering.astype(jnp.bfloat16)
    token_ids = jnp.arange(row_count, dtype=jnp.int32)
    causal = token_ids[None, :] <= token_ids[:, None]
    log_gap = jnp.where(causal[None], cumul[:, :, None] - cumul[:, None, :], -jnp.inf)
    raw_scores = jnp.einsum("thd,shd->hts", queries, keys_here, preferred_element_type=jnp.float32)
    gated = (raw_scores * jnp.exp(log_gap)).astype(jnp.bfloat16)
    inner = jnp.einsum("hts,shd->thd", gated, vals_here, preferred_element_type=jnp.float32)
    outer = (
        jnp.einsum("thd,hde->the", queries, state_low, preferred_element_type=jnp.float32)
        * jnp.exp(cumul).T[:, :, None]
    )
    raw_out = inner + outer
    mean_sq = jnp.mean(raw_out * raw_out, axis=2, keepdims=True)
    normed = raw_out * lax.rsqrt(mean_sq + 1e-06) * norm_gain.reshape(heads_dev, head_width)[None]
    return normed.astype(jnp.bfloat16).reshape(row_count, heads_dev * head_width)


def to_heads(arrays, parts):
    rows, width = arrays[0].shape
    chunk = width // parts
    send = jnp.stack([a.reshape(rows, parts, chunk) for a in arrays], axis=1)
    send = send.transpose(2, 1, 0, 3)
    got = lax.all_to_all(send, "head", split_axis=0, concat_axis=0, tiled=True)
    return got.transpose(1, 0, 2, 3).reshape(len(arrays), parts * rows, chunk)


def to_tokens(arrays, parts):
    rows, chunk = arrays[0].shape
    send = jnp.stack([a.reshape(parts, rows // parts, chunk) for a in arrays], axis=1)
    got = lax.all_to_all(send, "head", split_axis=0, concat_axis=0, tiled=True)
    return got.transpose(1, 2, 0, 3).reshape(len(arrays), rows // parts, parts * chunk)


def per_device(
    q_soft, k_soft, v_soft, q_light, k_light, v_light, decay_log, norm_gain, doc_lengths
):
    parts = lax.axis_size("head")
    moved = to_heads([k_soft, v_soft, q_soft, q_light, k_light, v_light], parts)
    kv_soft = moved[:2]
    rest = moved[2:]
    heads_dev = decay_log.shape[0]
    row_count = kv_soft.shape[1]
    head_width = kv_soft.shape[2] // heads_dev
    light_out = lightning(
        rest[1], rest[2], rest[3], decay_log, norm_gain, row_count, heads_dev, head_width
    )
    soft_out = soft_attention(rest[0], kv_soft, doc_lengths, row_count, heads_dev, head_width)
    returned = to_tokens([soft_out, light_out], parts)
    return (returned[0], returned[1])


def solution(mesh):
    in_specs = (
        P(("ctx", "head"), None),
        P(("ctx", "head"), None),
        P(("ctx", "head"), None),
        P(("ctx", "head"), None),
        P(("ctx", "head"), None),
        P(("ctx", "head"), None),
        P("head", "ctx"),
        P("head"),
        P(),
    )
    out_specs = (P(("ctx", "head"), None), P(("ctx", "head"), None))
    return jax.shard_map(
        per_device, mesh=mesh, in_specs=in_specs, out_specs=out_specs, check_vma=False
    )
```

```python
from functools import partial

import jax
import jax.numpy as jnp
from jax import lax
from jax.experimental import pallas as pl
from jax.sharding import PartitionSpec as P

DOC_REACH = 8


def shifted(block, axis, distance):
    size = lax.axis_size(axis)
    route = [(i, (i + distance) % size) for i in range(size)]
    return lax.ppermute(block, axis, route)


def doc_index(positions, starts):
    return jnp.sum((positions[:, None] >= starts[None, :]).astype(jnp.int32), axis=1) - 1


def online_block_kernel(
    masked, q_doc, k_doc, q_pos, k_pos, q_ref, kv_ref, m_in, l_in, acc_in, m_out, l_out, acc_out
):
    heads_dev = m_in.shape[0]
    head_width = q_ref.shape[1] // heads_dev
    k_ref = kv_ref.at[0]
    v_ref = kv_ref.at[1]
    allowed = (q_doc[:, :1] == k_doc[:1, :]) & (k_pos[:1, :] <= q_pos[:, :1])
    for h in range(heads_dev):
        cols = slice(h * head_width, (h + 1) * head_width)
        scores = lax.dot_general(
            q_ref[:, cols],
            k_ref[:, cols],
            (((1,), (1,)), ((), ())),
            preferred_element_type=jnp.float32,
        )
        scores = scores * (1.0 / head_width**0.5)
        if masked:
            scores = jnp.where(allowed, scores, -1e30)
        run_max = m_in[h][:, :1]
        new_max = jnp.maximum(run_max, jnp.max(scores, axis=1, keepdims=True))
        correction = jnp.exp(run_max - new_max)
        probs = jnp.exp(scores - new_max)
        if masked:
            probs = jnp.where(allowed, probs, 0.0)
        new_total = l_in[h][:, :1] * correction + jnp.sum(probs, axis=1, keepdims=True)
        product = jnp.dot(
            probs.astype(jnp.bfloat16), v_ref[:, cols], preferred_element_type=jnp.float32
        )
        acc_out[:, cols] = acc_in[:, cols] * correction + product
        m_out[h] = jnp.broadcast_to(new_max, m_out.shape[1:])
        l_out[h] = jnp.broadcast_to(new_total, l_out.shape[1:])


def online_block(running, kv_pair, queries, query_doc, query_pos, key_doc, key_pos, masked=True):
    run_max, run_total, run_acc = running
    rows, width = queries.shape
    heads_dev = run_max.shape[0]
    flops = 4 * rows * rows * width
    return pl.pallas_call(
        partial(online_block_kernel, masked),
        out_shape=(
            jax.ShapeDtypeStruct(run_max.shape, jnp.float32),
            jax.ShapeDtypeStruct(run_total.shape, jnp.float32),
            jax.ShapeDtypeStruct(run_acc.shape, jnp.float32),
        ),
        input_output_aliases={6: 0, 7: 1, 8: 2},
        cost_estimate=pl.CostEstimate(
            flops=flops, transcendentals=heads_dev * rows * rows, bytes_accessed=6 * rows * width * 4
        ),
    )(
        query_doc,
        key_doc,
        query_pos,
        key_pos,
        queries,
        kv_pair,
        run_max,
        run_total,
        run_acc,
    )


def soft_attention(q_rows, kv_pair, doc_lengths, row_count, heads_dev, head_width):
    size = lax.axis_size("ctx")
    own_index = lax.axis_index("ctx")
    reach = min(DOC_REACH, size - 1)
    forward_steps = (reach + 1) // 2
    starts = jnp.cumsum(doc_lengths) - doc_lengths
    query_pos = own_index * row_count + jnp.arange(row_count, dtype=jnp.int32)
    query_doc = doc_index(query_pos, starts)
    lanes = 128
    query_doc_wide = jnp.broadcast_to(query_doc[:, None], (row_count, lanes))
    query_pos_wide = jnp.broadcast_to(query_pos[:, None], (row_count, lanes))
    running = (
        jnp.full((heads_dev, row_count, lanes), -1e30, jnp.float32),
        jnp.zeros((heads_dev, row_count, lanes), jnp.float32),
        jnp.zeros((row_count, heads_dev * head_width), jnp.float32),
    )

    def absorb(running, block, source, masked=True):
        key_pos = source * row_count + jnp.arange(row_count, dtype=jnp.int32)
        key_doc = doc_index(key_pos, starts)
        return online_block(
            running,
            block,
            q_rows,
            query_doc_wide,
            query_pos_wide,
            jnp.broadcast_to(key_doc[None, :], (8, row_count)),
            jnp.broadcast_to(key_pos[None, :], (8, row_count)),
            masked,
        )

    def absorb_if_needed(running, block, offset):
        source = own_index - offset
        last_doc = doc_index(jnp.full((1,), source * row_count + row_count - 1, jnp.int32), starts)[
            0
        ]
        first_doc = doc_index(jnp.full((1,), source * row_count, jnp.int32), starts)[0]
        needed = (source >= 0) & (last_doc == query_doc[0])
        whole = (first_doc == query_doc[0]) & (query_doc[-1] == query_doc[0])
        branch = jnp.where(needed, jnp.where(whole, 2, 1), 0)
        return lax.switch(
            branch,
            [
                lambda r: r,
                lambda r: absorb(r, block, source),
                lambda r: absorb(r, block, source, masked=False),
            ],
            running,
        )

    fwd_offsets = list(range(1, forward_steps + 1))
    bwd_offsets = list(range(reach, forward_steps, -1))
    running = absorb(running, kv_pair, own_index)
    ahead = shifted(kv_pair, "ctx", 1)
    behind = shifted(kv_pair, "ctx", reach) if bwd_offsets else None
    for i in range(max(len(fwd_offsets), len(bwd_offsets))):
        ahead_next = shifted(ahead, "ctx", 1) if i + 1 < len(fwd_offsets) else None
        behind_next = shifted(behind, "ctx", -1) if i + 1 < len(bwd_offsets) else None
        if i < len(fwd_offsets):
            running = absorb_if_needed(running, ahead, fwd_offsets[i])
        if i < len(bwd_offsets):
            running = absorb_if_needed(running, behind, bwd_offsets[i])
        ahead_next, behind_next, running = lax.optimization_barrier(
            (ahead_next, behind_next, running)
        )
        ahead, behind = ahead_next, behind_next
    run_max, run_total, run_acc = running
    totals = run_total[:, :, 0].T
    mixed = run_acc.reshape(row_count, heads_dev, head_width) / totals[:, :, None]
    return mixed.astype(jnp.bfloat16).reshape(row_count, heads_dev * head_width)


def lightning(q_rows, k_rows, v_rows, decay_log, norm_gain, row_count, heads_dev, head_width):
    size = lax.axis_size("ctx")
    own_index = lax.axis_index("ctx")
    cumul = jnp.cumsum(decay_log, axis=1)
    block_end = cumul[:, -1:]
    queries = q_rows.reshape(row_count, heads_dev, head_width)
    keys_here = k_rows.reshape(row_count, heads_dev, head_width)
    vals_here = v_rows.reshape(row_count, heads_dev, head_width)
    weighted = (keys_here * jnp.exp(block_end - cumul).T[:, :, None]).astype(jnp.bfloat16)
    update = jnp.einsum("thd,the->hde", weighted, vals_here, preferred_element_type=jnp.float32)
    end_hi = block_end.astype(jnp.bfloat16)
    end_lo = (block_end - end_hi.astype(jnp.float32)).astype(jnp.bfloat16)
    extra = jnp.zeros((heads_dev, 16, head_width), jnp.bfloat16)
    extra = extra.at[:, 0, :].set(jnp.broadcast_to(end_hi, (heads_dev, head_width)))
    extra = extra.at[:, 1, :].set(jnp.broadcast_to(end_lo, (heads_dev, head_width)))
    packed = jnp.concatenate([update.astype(jnp.bfloat16), extra], axis=1)
    gathered = lax.all_gather(packed, "ctx")
    ends = gathered[:, :, head_width, 0].astype(jnp.float32) + gathered[
        :, :, head_width + 1, 0
    ].astype(jnp.float32)
    blocks = jnp.arange(size, dtype=jnp.int32)
    between = (blocks[:, None] < blocks[None, :]) & (blocks[None, :] < own_index)
    exponent = jnp.einsum(
        "cb,bh->ch", between.astype(jnp.float32), ends, precision=lax.Precision.HIGHEST
    )
    weight = jnp.where((blocks < own_index)[:, None], jnp.exp(exponent), 0.0)
    entering = jnp.einsum(
        "ch,chde->hde",
        weight,
        gathered[:, :, :head_width, :].astype(jnp.float32),
        precision=lax.Precision.HIGHEST,
    )
    state_low = entering.astype(jnp.bfloat16)
    token_ids = jnp.arange(row_count, dtype=jnp.int32)
    causal = token_ids[None, :] <= token_ids[:, None]
    log_gap = jnp.where(causal[None], cumul[:, :, None] - cumul[:, None, :], -jnp.inf)
    raw_scores = jnp.einsum("thd,shd->hts", queries, keys_here, preferred_element_type=jnp.float32)
    gated = (raw_scores * jnp.exp(log_gap)).astype(jnp.bfloat16)
    inner = jnp.einsum("hts,shd->thd", gated, vals_here, preferred_element_type=jnp.float32)
    outer = (
        jnp.einsum("thd,hde->the", queries, state_low, preferred_element_type=jnp.float32)
        * jnp.exp(cumul).T[:, :, None]
    )
    raw_out = inner + outer
    mean_sq = jnp.mean(raw_out * raw_out, axis=2, keepdims=True)
    normed = raw_out * lax.rsqrt(mean_sq + 1e-06) * norm_gain.reshape(heads_dev, head_width)[None]
    return normed.astype(jnp.bfloat16).reshape(row_count, heads_dev * head_width)


def to_heads(arrays, parts):
    rows, width = arrays[0].shape
    chunk = width // parts
    send = jnp.stack([a.reshape(rows, parts, chunk) for a in arrays], axis=1)
    send = send.transpose(2, 1, 0, 3)
    got = lax.all_to_all(send, "head", split_axis=0, concat_axis=0, tiled=True)
    return got.transpose(1, 0, 2, 3).reshape(len(arrays), parts * rows, chunk)


def to_tokens(arrays, parts):
    rows, chunk = arrays[0].shape
    send = jnp.stack([a.reshape(parts, rows // parts, chunk) for a in arrays], axis=1)
    got = lax.all_to_all(send, "head", split_axis=0, concat_axis=0, tiled=True)
    return got.transpose(1, 2, 0, 3).reshape(len(arrays), rows // parts, parts * chunk)


def per_device(
    q_soft, k_soft, v_soft, q_light, k_light, v_light, decay_log, norm_gain, doc_lengths
):
    parts = lax.axis_size("head")
    moved = to_heads([k_soft, v_soft, q_soft, q_light, k_light, v_light], parts)
    kv_soft = moved[:2]
    rest = moved[2:]
    heads_dev = decay_log.shape[0]
    row_count = kv_soft.shape[1]
    head_width = kv_soft.shape[2] // heads_dev
    light_out = lightning(
        rest[1], rest[2], rest[3], decay_log, norm_gain, row_count, heads_dev, head_width
    )
    soft_out = soft_attention(rest[0], kv_soft, doc_lengths, row_count, heads_dev, head_width)
    returned = to_tokens([soft_out, light_out], parts)
    return (returned[0], returned[1])


def solution(mesh):
    in_specs = (
        P(("ctx", "head"), None),
        P(("ctx", "head"), None),
        P(("ctx", "head"), None),
        P(("ctx", "head"), None),
        P(("ctx", "head"), None),
        P(("ctx", "head"), None),
        P("head", "ctx"),
        P("head"),
        P(),
    )
    out_specs = (P(("ctx", "head"), None), P(("ctx", "head"), None))
    return jax.shard_map(
        per_device, mesh=mesh, in_specs=in_specs, out_specs=out_specs, check_vma=False
    )
```

```python
from functools import partial

import jax
import jax.numpy as jnp
from jax import lax
from jax.experimental import pallas as pl
from jax.sharding import PartitionSpec as P

DOC_REACH = 8


def shifted(block, axis, distance):
    size = lax.axis_size(axis)
    route = [(i, (i + distance) % size) for i in range(size)]
    return lax.ppermute(block, axis, route)


def doc_index(positions, starts):
    return jnp.sum((positions[:, None] >= starts[None, :]).astype(jnp.int32), axis=1) - 1


def online_block_kernel(
    q_doc, k_doc, q_pos, k_pos, q_ref, kv_ref, m_in, l_in, acc_in, m_out, l_out, acc_out
):
    heads_dev = m_in.shape[0]
    head_width = q_ref.shape[1] // heads_dev
    k_ref = kv_ref.at[0]
    v_ref = kv_ref.at[1]
    allowed = (q_doc[:, :1] == k_doc[:1, :]) & (k_pos[:1, :] <= q_pos[:, :1])
    for h in range(heads_dev):
        cols = slice(h * head_width, (h + 1) * head_width)
        scores = lax.dot_general(
            q_ref[:, cols],
            k_ref[:, cols],
            (((1,), (1,)), ((), ())),
            preferred_element_type=jnp.float32,
        )
        scores = jnp.where(allowed, scores * (1.0 / head_width**0.5), -1e30)
        run_max = m_in[h][:, :1]
        new_max = jnp.maximum(run_max, jnp.max(scores, axis=1, keepdims=True))
        correction = jnp.exp(run_max - new_max)
        probs = jnp.where(allowed, jnp.exp(scores - new_max), 0.0)
        new_total = l_in[h][:, :1] * correction + jnp.sum(probs, axis=1, keepdims=True)
        product = jnp.dot(
            probs.astype(jnp.bfloat16), v_ref[:, cols], preferred_element_type=jnp.float32
        )
        acc_out[:, cols] = acc_in[:, cols] * correction + product
        m_out[h] = jnp.broadcast_to(new_max, m_out.shape[1:])
        l_out[h] = jnp.broadcast_to(new_total, l_out.shape[1:])


def online_block(running, kv_pair, queries, query_doc, query_pos, key_doc, key_pos):
    run_max, run_total, run_acc = running
    rows, width = queries.shape
    heads_dev = run_max.shape[0]
    flops = 4 * rows * rows * width
    return pl.pallas_call(
        online_block_kernel,
        out_shape=(
            jax.ShapeDtypeStruct(run_max.shape, jnp.float32),
            jax.ShapeDtypeStruct(run_total.shape, jnp.float32),
            jax.ShapeDtypeStruct(run_acc.shape, jnp.float32),
        ),
        input_output_aliases={6: 0, 7: 1, 8: 2},
        cost_estimate=pl.CostEstimate(
            flops=flops, transcendentals=heads_dev * rows * rows, bytes_accessed=6 * rows * width * 4
        ),
    )(
        query_doc,
        key_doc,
        query_pos,
        key_pos,
        queries,
        kv_pair,
        run_max,
        run_total,
        run_acc,
    )


def soft_attention(q_rows, kv_pair, doc_lengths, row_count, heads_dev, head_width):
    size = lax.axis_size("ctx")
    own_index = lax.axis_index("ctx")
    reach = min(DOC_REACH, size - 1)
    forward_steps = (reach + 1) // 2
    starts = jnp.cumsum(doc_lengths) - doc_lengths
    query_pos = own_index * row_count + jnp.arange(row_count, dtype=jnp.int32)
    query_doc = doc_index(query_pos, starts)
    lanes = 128
    query_doc_wide = jnp.broadcast_to(query_doc[:, None], (row_count, lanes))
    query_pos_wide = jnp.broadcast_to(query_pos[:, None], (row_count, lanes))
    running = (
        jnp.full((heads_dev, row_count, lanes), -1e30, jnp.float32),
        jnp.zeros((heads_dev, row_count, lanes), jnp.float32),
        jnp.zeros((row_count, heads_dev * head_width), jnp.float32),
    )

    def absorb(running, block, source):
        key_pos = source * row_count + jnp.arange(row_count, dtype=jnp.int32)
        key_doc = doc_index(key_pos, starts)
        return online_block(
            running,
            block,
            q_rows,
            query_doc_wide,
            query_pos_wide,
            jnp.broadcast_to(key_doc[None, :], (8, row_count)),
            jnp.broadcast_to(key_pos[None, :], (8, row_count)),
        )

    def absorb_if_needed(running, block, offset):
        source = own_index - offset
        last_doc = doc_index(jnp.full((1,), source * row_count + row_count - 1, jnp.int32), starts)[
            0
        ]
        needed = (source >= 0) & (last_doc == query_doc[0])
        return lax.cond(
            needed, lambda r: absorb(r, block, source), lambda r: r, running
        )

    fwd_offsets = list(range(1, forward_steps + 1))
    bwd_offsets = list(range(reach, forward_steps, -1))
    running = absorb(running, kv_pair, own_index)
    ahead = shifted(kv_pair, "ctx", 1)
    behind = shifted(kv_pair, "ctx", reach) if bwd_offsets else None
    for i in range(max(len(fwd_offsets), len(bwd_offsets))):
        if i == 0:
            ahead, running = lax.optimization_barrier((ahead, running))
        ahead_next = shifted(ahead, "ctx", 1) if i + 1 < len(fwd_offsets) else None
        behind_next = shifted(behind, "ctx", -1) if i + 1 < len(bwd_offsets) else None
        if i < len(fwd_offsets):
            running = absorb_if_needed(running, ahead, fwd_offsets[i])
        if i < len(bwd_offsets):
            running = absorb_if_needed(running, behind, bwd_offsets[i])
        ahead_next, behind_next, running = lax.optimization_barrier(
            (ahead_next, behind_next, running)
        )
        ahead, behind = ahead_next, behind_next
    run_max, run_total, run_acc = running
    totals = run_total[:, :, 0].T
    mixed = run_acc.reshape(row_count, heads_dev, head_width) / totals[:, :, None]
    return mixed.astype(jnp.bfloat16).reshape(row_count, heads_dev * head_width)


def lightning(q_rows, k_rows, v_rows, decay_log, norm_gain, row_count, heads_dev, head_width):
    size = lax.axis_size("ctx")
    own_index = lax.axis_index("ctx")
    cumul = jnp.cumsum(decay_log, axis=1)
    block_end = cumul[:, -1:]
    queries = q_rows.reshape(row_count, heads_dev, head_width)
    keys_here = k_rows.reshape(row_count, heads_dev, head_width)
    vals_here = v_rows.reshape(row_count, heads_dev, head_width)
    weighted = (keys_here * jnp.exp(block_end - cumul).T[:, :, None]).astype(jnp.bfloat16)
    update = jnp.einsum("thd,the->hde", weighted, vals_here, preferred_element_type=jnp.float32)
    end_hi = block_end.astype(jnp.bfloat16)
    end_lo = (block_end - end_hi.astype(jnp.float32)).astype(jnp.bfloat16)
    extra = jnp.zeros((heads_dev, 16, head_width), jnp.bfloat16)
    extra = extra.at[:, 0, :].set(jnp.broadcast_to(end_hi, (heads_dev, head_width)))
    extra = extra.at[:, 1, :].set(jnp.broadcast_to(end_lo, (heads_dev, head_width)))
    packed = jnp.concatenate([update.astype(jnp.bfloat16), extra], axis=1)
    gathered = lax.all_gather(packed, "ctx")
    ends = gathered[:, :, head_width, 0].astype(jnp.float32) + gathered[
        :, :, head_width + 1, 0
    ].astype(jnp.float32)
    blocks = jnp.arange(size, dtype=jnp.int32)
    between = (blocks[:, None] < blocks[None, :]) & (blocks[None, :] < own_index)
    exponent = jnp.einsum(
        "cb,bh->ch", between.astype(jnp.float32), ends, precision=lax.Precision.HIGHEST
    )
    weight = jnp.where((blocks < own_index)[:, None], jnp.exp(exponent), 0.0)
    entering = jnp.einsum(
        "ch,chde->hde",
        weight,
        gathered[:, :, :head_width, :].astype(jnp.float32),
        precision=lax.Precision.HIGHEST,
    )
    state_low = entering.astype(jnp.bfloat16)
    token_ids = jnp.arange(row_count, dtype=jnp.int32)
    causal = token_ids[None, :] <= token_ids[:, None]
    log_gap = jnp.where(causal[None], cumul[:, :, None] - cumul[:, None, :], -jnp.inf)
    raw_scores = jnp.einsum("thd,shd->hts", queries, keys_here, preferred_element_type=jnp.float32)
    gated = (raw_scores * jnp.exp(log_gap)).astype(jnp.bfloat16)
    inner = jnp.einsum("hts,shd->thd", gated, vals_here, preferred_element_type=jnp.float32)
    outer = (
        jnp.einsum("thd,hde->the", queries, state_low, preferred_element_type=jnp.float32)
        * jnp.exp(cumul).T[:, :, None]
    )
    raw_out = inner + outer
    mean_sq = jnp.mean(raw_out * raw_out, axis=2, keepdims=True)
    normed = raw_out * lax.rsqrt(mean_sq + 1e-06) * norm_gain.reshape(heads_dev, head_width)[None]
    return normed.astype(jnp.bfloat16).reshape(row_count, heads_dev * head_width)


def to_heads(arrays, parts):
    rows, width = arrays[0].shape
    chunk = width // parts
    send = jnp.stack([a.reshape(rows, parts, chunk) for a in arrays], axis=1)
    send = send.transpose(2, 1, 0, 3)
    got = lax.all_to_all(send, "head", split_axis=0, concat_axis=0, tiled=True)
    return got.transpose(1, 0, 2, 3).reshape(len(arrays), parts * rows, chunk)


def to_tokens(arrays, parts):
    rows, chunk = arrays[0].shape
    send = jnp.stack([a.reshape(parts, rows // parts, chunk) for a in arrays], axis=1)
    got = lax.all_to_all(send, "head", split_axis=0, concat_axis=0, tiled=True)
    return got.transpose(1, 2, 0, 3).reshape(len(arrays), rows // parts, parts * chunk)


def per_device(
    q_soft, k_soft, v_soft, q_light, k_light, v_light, decay_log, norm_gain, doc_lengths
):
    parts = lax.axis_size("head")
    moved = to_heads([k_soft, v_soft, q_soft, q_light, k_light, v_light], parts)
    kv_soft = moved[:2]
    rest = moved[2:]
    heads_dev = decay_log.shape[0]
    row_count = kv_soft.shape[1]
    head_width = kv_soft.shape[2] // heads_dev
    light_out = lightning(
        rest[1], rest[2], rest[3], decay_log, norm_gain, row_count, heads_dev, head_width
    )
    soft_out = soft_attention(rest[0], kv_soft, doc_lengths, row_count, heads_dev, head_width)
    returned = to_tokens([soft_out, light_out], parts)
    return (returned[0], returned[1])


def solution(mesh):
    in_specs = (
        P(("ctx", "head"), None),
        P(("ctx", "head"), None),
        P(("ctx", "head"), None),
        P(("ctx", "head"), None),
        P(("ctx", "head"), None),
        P(("ctx", "head"), None),
        P("head", "ctx"),
        P("head"),
        P(),
    )
    out_specs = (P(("ctx", "head"), None), P(("ctx", "head"), None))
    return jax.shard_map(
        per_device, mesh=mesh, in_specs=in_specs, out_specs=out_specs, check_vma=False
    )
```

```python
from functools import partial

import jax
import jax.numpy as jnp
from jax import lax
from jax.experimental import pallas as pl
from jax.sharding import PartitionSpec as P

DOC_REACH = 8


def shifted(block, axis, distance):
    size = lax.axis_size(axis)
    route = [(i, (i + distance) % size) for i in range(size)]
    return lax.ppermute(block, axis, route)


def doc_index(positions, starts):
    return jnp.sum((positions[:, None] >= starts[None, :]).astype(jnp.int32), axis=1) - 1


def online_block_kernel(
    q_doc, k_doc, q_pos, k_pos, q_ref, kv_ref, m_in, l_in, acc_in, m_out, l_out, acc_out
):
    heads_dev = m_in.shape[0]
    head_width = q_ref.shape[1] // heads_dev
    k_ref = kv_ref.at[0]
    v_ref = kv_ref.at[1]
    allowed = (q_doc[:, :1] == k_doc[:1, :]) & (k_pos[:1, :] <= q_pos[:, :1])
    for h in range(heads_dev):
        cols = slice(h * head_width, (h + 1) * head_width)
        scores = lax.dot_general(
            q_ref[:, cols],
            k_ref[:, cols],
            (((1,), (1,)), ((), ())),
            preferred_element_type=jnp.float32,
        )
        scores = jnp.where(allowed, scores * (1.0 / head_width**0.5), -1e30)
        run_max = m_in[h][:, :1]
        new_max = jnp.maximum(run_max, jnp.max(scores, axis=1, keepdims=True))
        correction = jnp.exp(run_max - new_max)
        probs = jnp.where(allowed, jnp.exp(scores - new_max), 0.0)
        new_total = l_in[h][:, :1] * correction + jnp.sum(probs, axis=1, keepdims=True)
        product = jnp.dot(
            probs.astype(jnp.bfloat16), v_ref[:, cols], preferred_element_type=jnp.float32
        )
        acc_out[:, cols] = acc_in[:, cols] * correction + product
        m_out[h] = jnp.broadcast_to(new_max, m_out.shape[1:])
        l_out[h] = jnp.broadcast_to(new_total, l_out.shape[1:])


def online_block(running, kv_pair, queries, query_doc, query_pos, key_doc, key_pos):
    run_max, run_total, run_acc = running
    rows, width = queries.shape
    heads_dev = run_max.shape[0]
    flops = 4 * rows * rows * width
    return pl.pallas_call(
        online_block_kernel,
        out_shape=(
            jax.ShapeDtypeStruct(run_max.shape, jnp.float32),
            jax.ShapeDtypeStruct(run_total.shape, jnp.float32),
            jax.ShapeDtypeStruct(run_acc.shape, jnp.float32),
        ),
        input_output_aliases={6: 0, 7: 1, 8: 2},
        cost_estimate=pl.CostEstimate(
            flops=flops, transcendentals=heads_dev * rows * rows, bytes_accessed=6 * rows * width * 4
        ),
    )(
        query_doc,
        key_doc,
        query_pos,
        key_pos,
        queries,
        kv_pair,
        run_max,
        run_total,
        run_acc,
    )


def soft_attention(q_rows, kv_pair, doc_lengths, row_count, heads_dev, head_width):
    size = lax.axis_size("ctx")
    own_index = lax.axis_index("ctx")
    reach = min(DOC_REACH, size - 1)
    forward_steps = (reach + 1) // 2
    starts = jnp.cumsum(doc_lengths) - doc_lengths
    query_pos = own_index * row_count + jnp.arange(row_count, dtype=jnp.int32)
    query_doc = doc_index(query_pos, starts)
    lanes = 128
    query_doc_wide = jnp.broadcast_to(query_doc[:, None], (row_count, lanes))
    query_pos_wide = jnp.broadcast_to(query_pos[:, None], (row_count, lanes))
    running = (
        jnp.full((heads_dev, row_count, lanes), -1e30, jnp.float32),
        jnp.zeros((heads_dev, row_count, lanes), jnp.float32),
        jnp.zeros((row_count, heads_dev * head_width), jnp.float32),
    )

    def absorb(running, block, source):
        key_pos = source * row_count + jnp.arange(row_count, dtype=jnp.int32)
        key_doc = doc_index(key_pos, starts)
        return online_block(
            running,
            block,
            q_rows,
            query_doc_wide,
            query_pos_wide,
            jnp.broadcast_to(key_doc[None, :], (8, row_count)),
            jnp.broadcast_to(key_pos[None, :], (8, row_count)),
        )

    def absorb_if_needed(running, block, offset):
        source = own_index - offset
        last_doc = doc_index(jnp.full((1,), source * row_count + row_count - 1, jnp.int32), starts)[
            0
        ]
        needed = (source >= 0) & (last_doc == query_doc[0])
        return lax.cond(
            needed, lambda r: absorb(r, block, source), lambda r: r, running
        )

    fwd_offsets = list(range(1, forward_steps + 1))
    bwd_offsets = list(range(reach, forward_steps, -1))
    running = absorb(running, kv_pair, own_index)
    ahead = shifted(kv_pair, "ctx", 1)
    behind = shifted(kv_pair, "ctx", reach) if bwd_offsets else None
    for i in range(max(len(fwd_offsets), len(bwd_offsets))):
        ahead_next = shifted(ahead, "ctx", 1) if i + 1 < len(fwd_offsets) else None
        behind_next = shifted(behind, "ctx", -1) if i + 1 < len(bwd_offsets) else None
        if i < len(fwd_offsets):
            running = absorb_if_needed(running, ahead, fwd_offsets[i])
            ahead_next, running = lax.optimization_barrier((ahead_next, running))
        if i < len(bwd_offsets):
            running = absorb_if_needed(running, behind, bwd_offsets[i])
            behind_next, running = lax.optimization_barrier((behind_next, running))
        ahead, behind = ahead_next, behind_next
    run_max, run_total, run_acc = running
    totals = run_total[:, :, 0].T
    mixed = run_acc.reshape(row_count, heads_dev, head_width) / totals[:, :, None]
    return mixed.astype(jnp.bfloat16).reshape(row_count, heads_dev * head_width)


def lightning(q_rows, k_rows, v_rows, decay_log, norm_gain, row_count, heads_dev, head_width):
    size = lax.axis_size("ctx")
    own_index = lax.axis_index("ctx")
    cumul = jnp.cumsum(decay_log, axis=1)
    block_end = cumul[:, -1:]
    queries = q_rows.reshape(row_count, heads_dev, head_width)
    keys_here = k_rows.reshape(row_count, heads_dev, head_width)
    vals_here = v_rows.reshape(row_count, heads_dev, head_width)
    weighted = (keys_here * jnp.exp(block_end - cumul).T[:, :, None]).astype(jnp.bfloat16)
    update = jnp.einsum("thd,the->hde", weighted, vals_here, preferred_element_type=jnp.float32)
    end_hi = block_end.astype(jnp.bfloat16)
    end_lo = (block_end - end_hi.astype(jnp.float32)).astype(jnp.bfloat16)
    extra = jnp.zeros((heads_dev, 16, head_width), jnp.bfloat16)
    extra = extra.at[:, 0, :].set(jnp.broadcast_to(end_hi, (heads_dev, head_width)))
    extra = extra.at[:, 1, :].set(jnp.broadcast_to(end_lo, (heads_dev, head_width)))
    packed = jnp.concatenate([update.astype(jnp.bfloat16), extra], axis=1)
    gathered = lax.all_gather(packed, "ctx")
    ends = gathered[:, :, head_width, 0].astype(jnp.float32) + gathered[
        :, :, head_width + 1, 0
    ].astype(jnp.float32)
    blocks = jnp.arange(size, dtype=jnp.int32)
    between = (blocks[:, None] < blocks[None, :]) & (blocks[None, :] < own_index)
    exponent = jnp.einsum(
        "cb,bh->ch", between.astype(jnp.float32), ends, precision=lax.Precision.HIGHEST
    )
    weight = jnp.where((blocks < own_index)[:, None], jnp.exp(exponent), 0.0)
    entering = jnp.einsum(
        "ch,chde->hde",
        weight,
        gathered[:, :, :head_width, :].astype(jnp.float32),
        precision=lax.Precision.HIGHEST,
    )
    state_low = entering.astype(jnp.bfloat16)
    token_ids = jnp.arange(row_count, dtype=jnp.int32)
    causal = token_ids[None, :] <= token_ids[:, None]
    log_gap = jnp.where(causal[None], cumul[:, :, None] - cumul[:, None, :], -jnp.inf)
    raw_scores = jnp.einsum("thd,shd->hts", queries, keys_here, preferred_element_type=jnp.float32)
    gated = (raw_scores * jnp.exp(log_gap)).astype(jnp.bfloat16)
    inner = jnp.einsum("hts,shd->thd", gated, vals_here, preferred_element_type=jnp.float32)
    outer = (
        jnp.einsum("thd,hde->the", queries, state_low, preferred_element_type=jnp.float32)
        * jnp.exp(cumul).T[:, :, None]
    )
    raw_out = inner + outer
    mean_sq = jnp.mean(raw_out * raw_out, axis=2, keepdims=True)
    normed = raw_out * lax.rsqrt(mean_sq + 1e-06) * norm_gain.reshape(heads_dev, head_width)[None]
    return normed.astype(jnp.bfloat16).reshape(row_count, heads_dev * head_width)


def to_heads(arrays, parts):
    rows, width = arrays[0].shape
    chunk = width // parts
    send = jnp.stack([a.reshape(rows, parts, chunk) for a in arrays], axis=1)
    send = send.transpose(2, 1, 0, 3)
    got = lax.all_to_all(send, "head", split_axis=0, concat_axis=0, tiled=True)
    return got.transpose(1, 0, 2, 3).reshape(len(arrays), parts * rows, chunk)


def to_tokens(arrays, parts):
    rows, chunk = arrays[0].shape
    send = jnp.stack([a.reshape(parts, rows // parts, chunk) for a in arrays], axis=1)
    got = lax.all_to_all(send, "head", split_axis=0, concat_axis=0, tiled=True)
    return got.transpose(1, 2, 0, 3).reshape(len(arrays), rows // parts, parts * chunk)


def per_device(
    q_soft, k_soft, v_soft, q_light, k_light, v_light, decay_log, norm_gain, doc_lengths
):
    parts = lax.axis_size("head")
    moved = to_heads([k_soft, v_soft, q_soft, q_light, k_light, v_light], parts)
    kv_soft = moved[:2]
    rest = moved[2:]
    heads_dev = decay_log.shape[0]
    row_count = kv_soft.shape[1]
    head_width = kv_soft.shape[2] // heads_dev
    light_out = lightning(
        rest[1], rest[2], rest[3], decay_log, norm_gain, row_count, heads_dev, head_width
    )
    soft_out = soft_attention(rest[0], kv_soft, doc_lengths, row_count, heads_dev, head_width)
    returned = to_tokens([soft_out, light_out], parts)
    return (returned[0], returned[1])


def solution(mesh):
    in_specs = (
        P(("ctx", "head"), None),
        P(("ctx", "head"), None),
        P(("ctx", "head"), None),
        P(("ctx", "head"), None),
        P(("ctx", "head"), None),
        P(("ctx", "head"), None),
        P("head", "ctx"),
        P("head"),
        P(),
    )
    out_specs = (P(("ctx", "head"), None), P(("ctx", "head"), None))
    return jax.shard_map(
        per_device, mesh=mesh, in_specs=in_specs, out_specs=out_specs, check_vma=False
    )
```

```python
from functools import partial

import jax
import jax.numpy as jnp
from jax import lax
from jax.experimental import pallas as pl
from jax.sharding import PartitionSpec as P

DOC_REACH = 8


def shifted(block, axis, distance):
    size = lax.axis_size(axis)
    route = [(i, (i + distance) % size) for i in range(size)]
    return lax.ppermute(block, axis, route)


def doc_index(positions, starts):
    return jnp.sum((positions[:, None] >= starts[None, :]).astype(jnp.int32), axis=1) - 1


def online_block_kernel(
    q_doc, k_doc, q_pos, k_pos, q_ref, kv_ref, m_in, l_in, acc_in, m_out, l_out, acc_out
):
    heads_dev = m_in.shape[0]
    head_width = q_ref.shape[1] // heads_dev
    k_ref = kv_ref.at[0]
    v_ref = kv_ref.at[1]
    allowed = (q_doc[:, :1] == k_doc[:1, :]) & (k_pos[:1, :] <= q_pos[:, :1])
    for h in range(heads_dev):
        cols = slice(h * head_width, (h + 1) * head_width)
        scores = lax.dot_general(
            q_ref[:, cols],
            k_ref[:, cols],
            (((1,), (1,)), ((), ())),
            preferred_element_type=jnp.float32,
        )
        scores = jnp.where(allowed, scores * (1.0 / head_width**0.5), -1e30)
        run_max = m_in[h][:, :1]
        new_max = jnp.maximum(run_max, jnp.max(scores, axis=1, keepdims=True))
        correction = jnp.exp(run_max - new_max)
        probs = jnp.where(allowed, jnp.exp(scores - new_max), 0.0)
        new_total = l_in[h][:, :1] * correction + jnp.sum(probs, axis=1, keepdims=True)
        product = jnp.dot(
            probs.astype(jnp.bfloat16), v_ref[:, cols], preferred_element_type=jnp.float32
        )
        acc_out[:, cols] = acc_in[:, cols] * correction + product
        m_out[h] = jnp.broadcast_to(new_max, m_out.shape[1:])
        l_out[h] = jnp.broadcast_to(new_total, l_out.shape[1:])


def online_block(running, kv_pair, queries, query_doc, query_pos, key_doc, key_pos):
    run_max, run_total, run_acc = running
    rows, width = queries.shape
    heads_dev = run_max.shape[0]
    flops = 4 * rows * rows * width
    return pl.pallas_call(
        online_block_kernel,
        out_shape=(
            jax.ShapeDtypeStruct(run_max.shape, jnp.float32),
            jax.ShapeDtypeStruct(run_total.shape, jnp.float32),
            jax.ShapeDtypeStruct(run_acc.shape, jnp.float32),
        ),
        input_output_aliases={6: 0, 7: 1, 8: 2},
        cost_estimate=pl.CostEstimate(
            flops=flops, transcendentals=heads_dev * rows * rows, bytes_accessed=6 * rows * width * 4
        ),
    )(
        query_doc,
        key_doc,
        query_pos,
        key_pos,
        queries,
        kv_pair,
        run_max,
        run_total,
        run_acc,
    )


def soft_attention(q_rows, kv_pair, doc_lengths, row_count, heads_dev, head_width, other):
    size = lax.axis_size("ctx")
    own_index = lax.axis_index("ctx")
    reach = min(DOC_REACH, size - 1)
    forward_steps = (reach + 1) // 2
    starts = jnp.cumsum(doc_lengths) - doc_lengths
    query_pos = own_index * row_count + jnp.arange(row_count, dtype=jnp.int32)
    query_doc = doc_index(query_pos, starts)
    lanes = 128
    query_doc_wide = jnp.broadcast_to(query_doc[:, None], (row_count, lanes))
    query_pos_wide = jnp.broadcast_to(query_pos[:, None], (row_count, lanes))
    running = (
        jnp.full((heads_dev, row_count, lanes), -1e30, jnp.float32),
        jnp.zeros((heads_dev, row_count, lanes), jnp.float32),
        jnp.zeros((row_count, heads_dev * head_width), jnp.float32),
    )

    def absorb(running, block, source):
        key_pos = source * row_count + jnp.arange(row_count, dtype=jnp.int32)
        key_doc = doc_index(key_pos, starts)
        return online_block(
            running,
            block,
            q_rows,
            query_doc_wide,
            query_pos_wide,
            jnp.broadcast_to(key_doc[None, :], (8, row_count)),
            jnp.broadcast_to(key_pos[None, :], (8, row_count)),
        )

    def absorb_if_needed(running, block, offset):
        source = own_index - offset
        last_doc = doc_index(jnp.full((1,), source * row_count + row_count - 1, jnp.int32), starts)[
            0
        ]
        needed = (source >= 0) & (last_doc == query_doc[0])
        return lax.cond(
            needed, lambda r: absorb(r, block, source), lambda r: r, running
        )

    fwd_offsets = list(range(1, forward_steps + 1))
    bwd_offsets = list(range(reach, forward_steps, -1))
    running = absorb(running, kv_pair, own_index)
    ahead = shifted(kv_pair, "ctx", 1)
    behind = shifted(kv_pair, "ctx", reach) if bwd_offsets else None
    for i in range(max(len(fwd_offsets), len(bwd_offsets))):
        ahead_next = shifted(ahead, "ctx", 1) if i + 1 < len(fwd_offsets) else None
        behind_next = shifted(behind, "ctx", -1) if i + 1 < len(bwd_offsets) else None
        if i < len(fwd_offsets):
            running = absorb_if_needed(running, ahead, fwd_offsets[i])
        if i < len(bwd_offsets):
            running = absorb_if_needed(running, behind, bwd_offsets[i])
        if i == max(len(fwd_offsets), len(bwd_offsets)) - 2:
            ahead_next, behind_next, running, other = lax.optimization_barrier(
                (ahead_next, behind_next, running, other)
            )
        else:
            ahead_next, behind_next, running = lax.optimization_barrier(
                (ahead_next, behind_next, running)
            )
        ahead, behind = ahead_next, behind_next
    run_max, run_total, run_acc = running
    totals = run_total[:, :, 0].T
    mixed = run_acc.reshape(row_count, heads_dev, head_width) / totals[:, :, None]
    return mixed.astype(jnp.bfloat16).reshape(row_count, heads_dev * head_width), other


def lightning(q_rows, k_rows, v_rows, decay_log, norm_gain, row_count, heads_dev, head_width):
    size = lax.axis_size("ctx")
    own_index = lax.axis_index("ctx")
    cumul = jnp.cumsum(decay_log, axis=1)
    block_end = cumul[:, -1:]
    queries = q_rows.reshape(row_count, heads_dev, head_width)
    keys_here = k_rows.reshape(row_count, heads_dev, head_width)
    vals_here = v_rows.reshape(row_count, heads_dev, head_width)
    weighted = (keys_here * jnp.exp(block_end - cumul).T[:, :, None]).astype(jnp.bfloat16)
    update = jnp.einsum("thd,the->hde", weighted, vals_here, preferred_element_type=jnp.float32)
    end_hi = block_end.astype(jnp.bfloat16)
    end_lo = (block_end - end_hi.astype(jnp.float32)).astype(jnp.bfloat16)
    extra = jnp.zeros((heads_dev, 16, head_width), jnp.bfloat16)
    extra = extra.at[:, 0, :].set(jnp.broadcast_to(end_hi, (heads_dev, head_width)))
    extra = extra.at[:, 1, :].set(jnp.broadcast_to(end_lo, (heads_dev, head_width)))
    packed = jnp.concatenate([update.astype(jnp.bfloat16), extra], axis=1)
    gathered = lax.all_gather(packed, "ctx")
    ends = gathered[:, :, head_width, 0].astype(jnp.float32) + gathered[
        :, :, head_width + 1, 0
    ].astype(jnp.float32)
    blocks = jnp.arange(size, dtype=jnp.int32)
    between = (blocks[:, None] < blocks[None, :]) & (blocks[None, :] < own_index)
    exponent = jnp.einsum(
        "cb,bh->ch", between.astype(jnp.float32), ends, precision=lax.Precision.HIGHEST
    )
    weight = jnp.where((blocks < own_index)[:, None], jnp.exp(exponent), 0.0)
    entering = jnp.einsum(
        "ch,chde->hde",
        weight,
        gathered[:, :, :head_width, :].astype(jnp.float32),
        precision=lax.Precision.HIGHEST,
    )
    state_low = entering.astype(jnp.bfloat16)
    token_ids = jnp.arange(row_count, dtype=jnp.int32)
    causal = token_ids[None, :] <= token_ids[:, None]
    log_gap = jnp.where(causal[None], cumul[:, :, None] - cumul[:, None, :], -jnp.inf)
    raw_scores = jnp.einsum("thd,shd->hts", queries, keys_here, preferred_element_type=jnp.float32)
    gated = (raw_scores * jnp.exp(log_gap)).astype(jnp.bfloat16)
    inner = jnp.einsum("hts,shd->thd", gated, vals_here, preferred_element_type=jnp.float32)
    outer = (
        jnp.einsum("thd,hde->the", queries, state_low, preferred_element_type=jnp.float32)
        * jnp.exp(cumul).T[:, :, None]
    )
    raw_out = inner + outer
    mean_sq = jnp.mean(raw_out * raw_out, axis=2, keepdims=True)
    normed = raw_out * lax.rsqrt(mean_sq + 1e-06) * norm_gain.reshape(heads_dev, head_width)[None]
    return normed.astype(jnp.bfloat16).reshape(row_count, heads_dev * head_width)


def to_heads(arrays, parts):
    rows, width = arrays[0].shape
    chunk = width // parts
    send = jnp.stack([a.reshape(rows, parts, chunk) for a in arrays], axis=1)
    send = send.transpose(2, 1, 0, 3)
    got = lax.all_to_all(send, "head", split_axis=0, concat_axis=0, tiled=True)
    return got.transpose(1, 0, 2, 3).reshape(len(arrays), parts * rows, chunk)


def to_tokens(arrays, parts):
    rows, chunk = arrays[0].shape
    send = jnp.stack([a.reshape(parts, rows // parts, chunk) for a in arrays], axis=1)
    got = lax.all_to_all(send, "head", split_axis=0, concat_axis=0, tiled=True)
    return got.transpose(1, 2, 0, 3).reshape(len(arrays), rows // parts, parts * chunk)


def per_device(
    q_soft, k_soft, v_soft, q_light, k_light, v_light, decay_log, norm_gain, doc_lengths
):
    parts = lax.axis_size("head")
    moved = to_heads([k_soft, v_soft, q_soft, q_light, k_light, v_light], parts)
    kv_soft = moved[:2]
    rest = moved[2:]
    heads_dev = decay_log.shape[0]
    row_count = kv_soft.shape[1]
    head_width = kv_soft.shape[2] // heads_dev
    light_out = lightning(
        rest[1], rest[2], rest[3], decay_log, norm_gain, row_count, heads_dev, head_width
    )
    soft_out, light_out = soft_attention(
        rest[0], kv_soft, doc_lengths, row_count, heads_dev, head_width, light_out
    )
    returned = to_tokens([soft_out, light_out], parts)
    return (returned[0], returned[1])


def solution(mesh):
    in_specs = (
        P(("ctx", "head"), None),
        P(("ctx", "head"), None),
        P(("ctx", "head"), None),
        P(("ctx", "head"), None),
        P(("ctx", "head"), None),
        P(("ctx", "head"), None),
        P("head", "ctx"),
        P("head"),
        P(),
    )
    out_specs = (P(("ctx", "head"), None), P(("ctx", "head"), None))
    return jax.shard_map(
        per_device, mesh=mesh, in_specs=in_specs, out_specs=out_specs, check_vma=False
    )
```
